256 devices in a mesh: subj: 16 (over x, y), gz: 4 (over z_hi, core), gy: 4 (over z_lo).
Axes of the slice: x: 4, y: 4, z: 8 (z_hi: 2, z_lo: 4; z = z_hi * 4 + z_lo), core: 2. Of those that a mesh axis runs over, the one named last changes fastest.
Arguments:
- subjects: float32 [16, 32, 32, 640], P('subj', 'gz', 'gy'), may hold values from -6 to 6
- templates: float32 [4, 32, 32, 640], P(None, 'gz', 'gy'), may hold values from -6 to 6
- group_of: int32 [16], replicated, may hold values from 0 to 3, as said below
- extents: int32 [16, 4], replicated, may hold values from 0 to 32, as said below
Outputs:
- new_templates: float32 [4, 32, 32, 640], P(None, 'gz', 'gy')
- velocity: float32 [3, 32, 32, 640], P(None, 'gz', 'gy')
The draws below stay inside these ranges and needn't reach their ends.
Inputs may be any that keep to these rules, and one draw needn't show every extreme that they name: `extents`: columns are z_lo, z_hi, y_lo, y_hi of one subject in whole-volume indices, with 1 <= z_lo < z_hi <= 32 and 0 <= y_lo < y_hi <= 32. `group_of`: subjects 0 and 1 are in different groups.
All inputs are finite; a program needn't handle non-finite values.
Results may differ from the reference program's by a relative error of at most 0.00002.
Values sent between devices are 32-bit elements; how exact they have to be, the bound alone decides.
No kernel may reach another device: no remote copies, remote signals or barrier semaphores. Data moves between devices by JAX's collectives and lax.ppermute only.
A program may use at most 64 MiB of HBM per device.

```python
from functools import partial
from functools import reduce
import jax
import jax.numpy as jnp
from jax import lax

X = 640
G = 4
SUBJ = 16
Z = 32
Y = 32


def draw_group_of(key, part):
    keys = jax.random.split(jax.random.fold_in(key, 29), 2)
    groups = jax.random.randint(keys[0], (SUBJ,), 0, G)
    step = jax.random.randint(keys[1], (), 1, G)
    groups = groups.at[1].set((groups[0] + step) % G)
    return groups.astype(jnp.int32)


def draw_extents(key, part):
    keys = jax.random.split(jax.random.fold_in(key, 17), 4)
    z_quarter = max(Z // 4, 1)
    y_quarter = max(Y // 4, 1)
    z_low = jax.random.randint(keys[0], (SUBJ,), 0, z_quarter)
    z_high = jax.random.randint(keys[1], (SUBJ,), 0, z_quarter)
    y_low = jax.random.randint(keys[2], (SUBJ,), 0, y_quarter)
    y_high = jax.random.randint(keys[3], (SUBJ,), 0, y_quarter)
    z_low = 1 + z_low - jnp.min(z_low)
    z_high = Z - (z_high - jnp.min(z_high))
    y_low = y_low - jnp.min(y_low)
    y_high = Y - (y_high - jnp.min(y_high))
    return jnp.stack([z_low, z_high, y_low, y_high], axis=1).astype(jnp.int32)


def level_of(key, dims, shards, low, high):
    def one(dim, parts):
        heights = jax.random.uniform(jax.random.fold_in(jax.random.fold_in(key, 6), dim), (parts,), jnp.float32, low / len(shards), high / len(shards))
        return jnp.repeat(jnp.exp(heights), dims[dim] // parts).reshape((-1,) + (1,) * (len(dims) - dim - 1))

    gain = one(*shards[0])
    for cut in shards[1:]:
        gain = gain * one(*cut)
    return gain


def normal_values(key, dims, scale, limit, cuts=(), kind=jnp.bfloat16):
    level = level_of(key, dims, cuts, -0.22, 0.18) if cuts else 1.0
    result = jax.random.normal(key, dims, jnp.float32) * scale * level
    return jnp.minimum(jnp.maximum(result, -limit), limit).astype(kind)


def setup_inputs(seed: int = 0) -> dict:
    arg_keys = jax.random.split(jax.random.key(seed), 5)
    return {
        "subjects": normal_values(arg_keys[0], (SUBJ, Z, Y, X), 1.0, 6.0, ((0, 16), (1, 4), (2, 4)), jnp.float32),
        "templates": normal_values(arg_keys[1], (G, Z, Y, X), 1.0, 6.0, ((1, 4), (2, 4)), jnp.float32),
        "group_of": draw_group_of(jax.random.fold_in(arg_keys[4], 71), 0),
        "extents": draw_extents(jax.random.fold_in(arg_keys[4], 71), 0),
    }


BOX_EPS = 1e-5
SPREAD = (0.0625, 0.25, 0.375, 0.25, 0.0625)


def add_pair(former, latter):
    return former + latter


def window_sum(volume, along_axis, length, extent):
    pieces = [lax.slice_in_dim(volume, offset, offset + length, axis=along_axis) for offset in range(extent)]
    return reduce(add_pair, pieces)


def weighted(volume, along_axis, length):
    pieces = [SPREAD[offset] * lax.slice_in_dim(volume, offset, offset + length, axis=along_axis) for offset in range(5)]
    return reduce(add_pair, pieces)


def box_local(padded, slab_depth, slab_rows):
    widened = jnp.pad(padded, ((0, 0), (0, 0), (4, 4)))
    along_x = window_sum(widened, 2, padded.shape[2], 9)
    along_y = window_sum(along_x, 1, slab_rows, 9)
    return window_sum(along_y, 0, slab_depth, 9)


def smooth_local(padded, slab_depth, slab_rows):
    widened = jnp.pad(padded, ((0, 0), (0, 0), (2, 2)))
    along_x = weighted(widened, 2, padded.shape[2])
    along_y = weighted(along_x, 1, slab_rows)
    return weighted(along_y, 0, slab_depth)


def template_stats(templ_pad, slab_depth, slab_rows):
    templ_mean = box_local(templ_pad, slab_depth, slab_rows) / 729.0
    templ_var = box_local(templ_pad * templ_pad, slab_depth, slab_rows) / 729.0 - templ_mean * templ_mean + BOX_EPS
    return templ_mean, templ_var


def region_masks(extents, z_index, y_index):
    inside_z = (z_index[None, :] >= extents[:, 0:1]) & (z_index[None, :] < extents[:, 1:2])
    inside_y = (y_index[None, :] >= extents[:, 2:3]) & (y_index[None, :] < extents[:, 3:4])
    return (inside_z[:, :, None] & inside_y[:, None, :]).astype(jnp.float32)


def subject_force(image_pad, templ_pad, templ_mean, templ_var, region_mask, slab_depth, slab_rows):
    mean_i = box_local(image_pad, slab_depth, slab_rows) / 729.0
    square_mean = box_local(image_pad * image_pad, slab_depth, slab_rows) / 729.0
    cross_mean = box_local(image_pad * templ_pad, slab_depth, slab_rows) / 729.0
    var_i = square_mean - mean_i * mean_i + BOX_EPS
    covariance = cross_mean - mean_i * templ_mean
    image_mid = image_pad[4:4 + slab_depth, 4:4 + slab_rows, :]
    templ_mid = templ_pad[4:4 + slab_depth, 4:4 + slab_rows, :]
    centred_i = image_mid - mean_i
    centred_t = templ_mid - templ_mean
    factor = region_mask * (2.0 * covariance / (var_i * templ_var)) * (centred_t - (covariance / var_i) * centred_i)
    grad_z = 0.5 * (image_pad[5:5 + slab_depth, 4:4 + slab_rows, :] - image_pad[3:3 + slab_depth, 4:4 + slab_rows, :])
    grad_y = 0.5 * (image_pad[4:4 + slab_depth, 5:5 + slab_rows, :] - image_pad[4:4 + slab_depth, 3:3 + slab_rows, :])
    side_pad = jnp.pad(image_mid, ((0, 0), (0, 0), (1, 1)))
    grad_x = 0.5 * (side_pad[:, :, 2:] - side_pad[:, :, :-2])
    force_field = jnp.stack([factor * grad_z, factor * grad_y, factor * grad_x])
    return force_field, region_mask * image_mid


def reference(subjects, templates, group_of, extents):
    slab_depth = subjects.shape[1]
    slab_rows = subjects.shape[2]
    margin = ((0, 0), (4, 4), (4, 4), (0, 0))
    templ_all = jnp.pad(templates, margin)
    templ_mean, templ_var = jax.vmap(partial(template_stats, slab_depth=slab_depth, slab_rows=slab_rows))(templ_all)
    z_index = jnp.arange(slab_depth, dtype=jnp.int32)
    y_index = jnp.arange(slab_rows, dtype=jnp.int32)
    all_masks = region_masks(extents, z_index, y_index)
    onehot = (group_of[:, None] == jnp.arange(G, dtype=jnp.int32)[None, :]).astype(jnp.float32)
    counts = jnp.sum(onehot[:, :, None, None] * all_masks[:, None], axis=0)

    def advance(totals, subject_index):
        group_index = group_of[subject_index]
        image_pad = jnp.pad(subjects[subject_index], margin[1:])
        region_mask = all_masks[subject_index][:, :, None]
        force_field, masked = subject_force(image_pad, templ_all[group_index], templ_mean[group_index], templ_var[group_index], region_mask, slab_depth, slab_rows)
        return (totals[0].at[group_index].add(masked), totals[1] + force_field), None

    start = (jnp.zeros(templates.shape, jnp.float32), jnp.zeros((3,) + subjects.shape[1:], jnp.float32))
    totals, unused = lax.scan(advance, start, jnp.arange(subjects.shape[0], dtype=jnp.int32))
    force_pad = jnp.pad(totals[1], ((0, 0), (2, 2), (2, 2), (0, 0)))
    velocity = jax.vmap(partial(smooth_local, slab_depth=slab_depth, slab_rows=slab_rows))(force_pad)
    new_templates = totals[0] / jnp.maximum(counts, 1.0)[..., None]
    return new_templates, velocity
```

```python
from functools import partial
from functools import reduce

import jax
import jax.numpy as jnp
from jax import lax
from jax.sharding import PartitionSpec as P

BOX_EPS = 1e-05
SPREAD = (0.0625, 0.25, 0.375, 0.25, 0.0625)


def padded_2(x, sides, width):
    for axis, dim in sides:
        peers, length = (lax.axis_size(axis), x.shape[dim])
        up = [(i, (i + 1) % peers) for i in range(peers - 1)]
        down = [(j, i) for i, j in up]
        last = lax.slice_in_dim(x, length - width, length, axis=dim)
        initial = lax.slice_in_dim(x, 0, width, axis=dim)
        before = lax.ppermute(last, axis, up)
        after = lax.ppermute(initial, axis, down)
        x = jnp.concatenate([before, x, after], axis=dim)
    return x


def add_pair(former, latter):
    return former + latter


def window_sum(volume, along_axis, length, extent):
    pieces = [
        lax.slice_in_dim(volume, offset, offset + length, axis=along_axis)
        for offset in range(extent)
    ]
    return reduce(add_pair, pieces)


def weighted(volume, along_axis, length):
    pieces = [
        SPREAD[offset] * lax.slice_in_dim(volume, offset, offset + length, axis=along_axis)
        for offset in range(5)
    ]
    return reduce(add_pair, pieces)


def box_local(padded, slab_depth, slab_rows):
    widened = jnp.pad(padded, ((0, 0), (0, 0), (4, 4)))
    along_x = window_sum(widened, 2, padded.shape[2], 9)
    along_y = window_sum(along_x, 1, slab_rows, 9)
    return window_sum(along_y, 0, slab_depth, 9)


def smooth_local(padded, slab_depth, slab_rows):
    widened = jnp.pad(padded, ((0, 0), (0, 0), (2, 2)))
    along_x = weighted(widened, 2, padded.shape[2])
    along_y = weighted(along_x, 1, slab_rows)
    return weighted(along_y, 0, slab_depth)


def template_stats(templ_pad, slab_depth, slab_rows):
    templ_mean = box_local(templ_pad, slab_depth, slab_rows) / 729.0
    templ_var = (
        box_local(templ_pad * templ_pad, slab_depth, slab_rows) / 729.0
        - templ_mean * templ_mean
        + BOX_EPS
    )
    return (templ_mean, templ_var)


def region_masks(extents, z_index, y_index):
    inside_z = (z_index[None, :] >= extents[:, 0:1]) & (z_index[None, :] < extents[:, 1:2])
    inside_y = (y_index[None, :] >= extents[:, 2:3]) & (y_index[None, :] < extents[:, 3:4])
    return (inside_z[:, :, None] & inside_y[:, None, :]).astype(jnp.float32)


def subject_force(image_pad, templ_pad, region_mask, slab_depth, slab_rows):
    templ_mean, templ_var = template_stats(templ_pad, slab_depth, slab_rows)
    mean_i = box_local(image_pad, slab_depth, slab_rows) / 729.0
    square_mean = box_local(image_pad * image_pad, slab_depth, slab_rows) / 729.0
    cross_mean = box_local(image_pad * templ_pad, slab_depth, slab_rows) / 729.0
    var_i = square_mean - mean_i * mean_i + BOX_EPS
    covariance = cross_mean - mean_i * templ_mean
    image_mid = image_pad[4 : 4 + slab_depth, 4 : 4 + slab_rows, :]
    templ_mid = templ_pad[4 : 4 + slab_depth, 4 : 4 + slab_rows, :]
    centred_i = image_mid - mean_i
    centred_t = templ_mid - templ_mean
    factor = (
        region_mask
        * (2.0 * covariance / (var_i * templ_var))
        * (centred_t - covariance / var_i * centred_i)
    )
    grad_z = 0.5 * (
        image_pad[5 : 5 + slab_depth, 4 : 4 + slab_rows, :]
        - image_pad[3 : 3 + slab_depth, 4 : 4 + slab_rows, :]
    )
    grad_y = 0.5 * (
        image_pad[4 : 4 + slab_depth, 5 : 5 + slab_rows, :]
        - image_pad[4 : 4 + slab_depth, 3 : 3 + slab_rows, :]
    )
    side_pad = jnp.pad(image_mid, ((0, 0), (0, 0), (1, 1)))
    grad_x = 0.5 * (side_pad[:, :, 2:] - side_pad[:, :, :-2])
    return jnp.stack([factor * grad_z, factor * grad_y, factor * grad_x])


def scatter_sum(pieces, axis):
    received = lax.all_to_all(pieces, axis, 0, 0, tiled=True)
    return received


def gather_all(part, axis):
    peers = lax.axis_size(axis)
    copies = jnp.broadcast_to(part[None], (peers,) + part.shape)
    return lax.all_to_all(copies, axis, 0, 0, tiled=True)


def local(subjects, templates, group_of, extents):
    local_subjects, slab_depth, slab_rows, cell_count = subjects.shape
    groups = templates.shape[0]
    peers = lax.axis_size("subj")
    cells = slab_depth * slab_rows * cell_count
    chunk = cells // peers
    smoother = jax.vmap(partial(smooth_local, slab_depth=slab_depth, slab_rows=slab_rows))
    first_subject = lax.axis_index("subj") * local_subjects
    own_groups = lax.dynamic_slice_in_dim(group_of, first_subject, local_subjects)
    own_templates = jnp.take(templates, own_groups, axis=0)
    z_index = lax.axis_index("gz") * slab_depth + jnp.arange(slab_depth, dtype=jnp.int32)
    y_index = lax.axis_index("gy") * slab_rows + jnp.arange(slab_rows, dtype=jnp.int32)
    all_masks = region_masks(extents, z_index, y_index)
    own_masks = lax.dynamic_slice_in_dim(all_masks, first_subject, local_subjects)
    onehot = (group_of[:, None] == jnp.arange(groups, dtype=jnp.int32)[None, :]).astype(jnp.float32)
    counts = jnp.sum(onehot[:, :, None, None] * all_masks[:, None], axis=0)
    denominator = jnp.maximum(counts, 1.0)[..., None]

    masked = own_masks[..., None] * subjects
    pieces = masked.reshape(local_subjects, peers, chunk).transpose(1, 0, 2)
    arrived = scatter_sum(pieces, "subj").reshape(peers * local_subjects, chunk)
    group_parts = jnp.stack(
        [
            jnp.sum(jnp.where((group_of == g)[:, None], arrived, 0.0), axis=0)
            for g in range(groups)
        ]
    )
    group_full = gather_all(group_parts, "subj")
    template_sum = group_full.transpose(1, 0, 2).reshape(templates.shape)
    new_templates = template_sum / denominator

    volumes = jnp.concatenate([own_templates, subjects], axis=0)
    padded = padded_2(volumes, (("gz", 1), ("gy", 2)), 4)
    templ_all = padded[:local_subjects]
    image_all = padded[local_subjects:]
    forces = jax.vmap(
        partial(subject_force, slab_depth=slab_depth, slab_rows=slab_rows)
    )(image_all, templ_all, own_masks[..., None])
    force_sum = jnp.sum(forces, axis=0)

    force_pieces = force_sum.reshape(3, peers, chunk).transpose(1, 0, 2)
    force_part = jnp.sum(scatter_sum(force_pieces, "subj"), axis=0)
    force_full = gather_all(force_part, "subj")
    velocity_sum = force_full.transpose(1, 0, 2).reshape(3, slab_depth, slab_rows, cell_count)
    summed_pad = padded_2(velocity_sum, (("gz", 1), ("gy", 2)), 2)
    velocity = smoother(summed_pad)
    return (new_templates, velocity)


def solution(mesh):
    in_specs = (P("subj", "gz", "gy", None), P(None, "gz", "gy", None), P(), P())
    out_specs = (P(None, "gz", "gy", None), P(None, "gz", "gy", None))
    return jax.shard_map(local, mesh=mesh, in_specs=in_specs, out_specs=out_specs, check_vma=False)
```

```python
from functools import partial
from functools import reduce

import jax
import jax.numpy as jnp
from jax import lax
from jax.sharding import PartitionSpec as P

BOX_EPS = 1e-05
SPREAD = (0.0625, 0.25, 0.375, 0.25, 0.0625)
REACH = 4
SPILL = 2


def rim(x, side, dim, width):
    length = x.shape[dim]
    if side < 0:
        return lax.slice_in_dim(x, length - width, length, axis=dim)
    if side > 0:
        return lax.slice_in_dim(x, 0, width, axis=dim)
    return x


def halo_exchange(x, width):
    nz, ny = (lax.axis_size("gz"), lax.axis_size("gy"))
    grid = {}
    for sz in (-1, 0, 1):
        for sy in (-1, 0, 1):
            if sz == 0 and sy == 0:
                grid[sz, sy] = x
                continue
            piece = rim(rim(x, sz, 1, width), sy, 2, width)
            perm = []
            for gz in range(nz):
                for gy in range(ny):
                    tz, ty = (gz - sz, gy - sy)
                    if 0 <= tz < nz and 0 <= ty < ny:
                        perm.append((gz * ny + gy, tz * ny + ty))
            grid[sz, sy] = lax.ppermute(piece, ("gz", "gy"), perm)
    bands = [
        jnp.concatenate([grid[sz, -1], grid[sz, 0], grid[sz, 1]], axis=2) for sz in (-1, 0, 1)
    ]
    return jnp.concatenate(bands, axis=1)


def add_pair(former, latter):
    return former + latter


def window_sum(volume, along_axis, length, extent):
    pieces = [
        lax.slice_in_dim(volume, offset, offset + length, axis=along_axis)
        for offset in range(extent)
    ]
    return reduce(add_pair, pieces)


def weighted(volume, along_axis, length):
    pieces = [
        SPREAD[offset] * lax.slice_in_dim(volume, offset, offset + length, axis=along_axis)
        for offset in range(5)
    ]
    return reduce(add_pair, pieces)


def box_local(padded, slab_depth, slab_rows):
    widened = jnp.pad(padded, ((0, 0), (0, 0), (4, 4)))
    along_x = window_sum(widened, 2, padded.shape[2], 9)
    along_y = window_sum(along_x, 1, slab_rows, 9)
    return window_sum(along_y, 0, slab_depth, 9)


def smooth_local(padded, slab_depth, slab_rows):
    widened = jnp.pad(padded, ((0, 0), (0, 0), (2, 2)))
    along_x = weighted(widened, 2, padded.shape[2])
    along_y = weighted(along_x, 1, slab_rows)
    return weighted(along_y, 0, slab_depth)


def template_stats(templ_pad, slab_depth, slab_rows):
    templ_mean = box_local(templ_pad, slab_depth, slab_rows) / 729.0
    templ_var = (
        box_local(templ_pad * templ_pad, slab_depth, slab_rows) / 729.0
        - templ_mean * templ_mean
        + BOX_EPS
    )
    return (templ_mean, templ_var)


def region_masks(extents, z_index, y_index):
    inside_z = (z_index[None, :] >= extents[:, 0:1]) & (z_index[None, :] < extents[:, 1:2])
    inside_y = (y_index[None, :] >= extents[:, 2:3]) & (y_index[None, :] < extents[:, 3:4])
    return (inside_z[:, :, None] & inside_y[:, None, :]).astype(jnp.float32)


def subject_force(image_pad, templ_pad, region_mask, in_grid, slab_depth, slab_rows):
    templ_mean, templ_var = template_stats(templ_pad, slab_depth, slab_rows)
    mean_i = box_local(image_pad, slab_depth, slab_rows) / 729.0
    square_mean = box_local(image_pad * image_pad, slab_depth, slab_rows) / 729.0
    cross_mean = box_local(image_pad * templ_pad, slab_depth, slab_rows) / 729.0
    var_i = square_mean - mean_i * mean_i + BOX_EPS
    covariance = cross_mean - mean_i * templ_mean
    image_mid = image_pad[4 : 4 + slab_depth, 4 : 4 + slab_rows, :]
    templ_mid = templ_pad[4 : 4 + slab_depth, 4 : 4 + slab_rows, :]
    centred_i = image_mid - mean_i
    centred_t = templ_mid - templ_mean
    factor = (
        region_mask
        * (2.0 * covariance / (var_i * templ_var))
        * (centred_t - covariance / var_i * centred_i)
    )
    grad_z = 0.5 * (
        image_pad[5 : 5 + slab_depth, 4 : 4 + slab_rows, :]
        - image_pad[3 : 3 + slab_depth, 4 : 4 + slab_rows, :]
    )
    grad_y = 0.5 * (
        image_pad[4 : 4 + slab_depth, 5 : 5 + slab_rows, :]
        - image_pad[4 : 4 + slab_depth, 3 : 3 + slab_rows, :]
    )
    side_pad = jnp.pad(image_mid, ((0, 0), (0, 0), (1, 1)))
    grad_x = 0.5 * (side_pad[:, :, 2:] - side_pad[:, :, :-2])
    force = jnp.stack([factor * grad_z, factor * grad_y, factor * grad_x])
    return jnp.where(in_grid[None], force, 0.0)


def local(subjects, templates, group_of, extents):
    local_subjects, slab_depth, slab_rows, cell_count = subjects.shape
    groups = templates.shape[0]
    peers = lax.axis_size("subj")
    cells = slab_depth * slab_rows * cell_count
    chunk = cells // peers
    depth_out, rows_out = (slab_depth + 2 * SPILL, slab_rows + 2 * SPILL)
    total_z, total_y = (slab_depth * lax.axis_size("gz"), slab_rows * lax.axis_size("gy"))
    first_subject = lax.axis_index("subj") * local_subjects
    own_groups = lax.dynamic_slice_in_dim(group_of, first_subject, local_subjects)
    own_templates = jnp.take(templates, own_groups, axis=0)
    z_start = lax.axis_index("gz") * slab_depth
    y_start = lax.axis_index("gy") * slab_rows
    z_index = z_start + jnp.arange(slab_depth, dtype=jnp.int32)
    y_index = y_start + jnp.arange(slab_rows, dtype=jnp.int32)
    all_masks = region_masks(extents, z_index, y_index)
    own_masks = lax.dynamic_slice_in_dim(all_masks, first_subject, local_subjects)
    onehot = (group_of[:, None] == jnp.arange(groups, dtype=jnp.int32)[None, :]).astype(jnp.float32)
    counts = jnp.sum(onehot[:, :, None, None] * all_masks[:, None], axis=0)
    denominator = jnp.maximum(counts, 1.0)[..., None]

    z_wide = z_start - SPILL + jnp.arange(depth_out, dtype=jnp.int32)
    y_wide = y_start - SPILL + jnp.arange(rows_out, dtype=jnp.int32)
    wide_masks = lax.dynamic_slice_in_dim(
        region_masks(extents, z_wide, y_wide), first_subject, local_subjects
    )
    in_grid = (
        ((z_wide >= 0) & (z_wide < total_z))[:, None, None]
        & ((y_wide >= 0) & (y_wide < total_y))[None, :, None]
    )

    volumes = jnp.concatenate([own_templates, subjects], axis=0)
    padded = halo_exchange(volumes, REACH + SPILL)
    templ_all = padded[:local_subjects]
    image_all = padded[local_subjects:]
    forces = jax.vmap(
        partial(subject_force, in_grid=in_grid, slab_depth=depth_out, slab_rows=rows_out)
    )(image_all, templ_all, wide_masks[..., None])
    force_sum = jnp.sum(forces, axis=0)
    smoother = jax.vmap(partial(smooth_local, slab_depth=slab_depth, slab_rows=slab_rows))
    velocity_part = smoother(force_sum)

    masked = own_masks[..., None] * subjects
    outgoing = jnp.concatenate(
        [masked.reshape(local_subjects, peers, chunk), velocity_part.reshape(3, peers, chunk)]
    ).transpose(1, 0, 2)
    arrived = lax.all_to_all(outgoing, "subj", 0, 0, tiled=True)
    images = arrived[:, :local_subjects].reshape(peers * local_subjects, chunk)
    group_parts = [
        jnp.sum(jnp.where((group_of == g)[:, None], images, 0.0), axis=0) for g in range(groups)
    ]
    velocity_chunk = jnp.sum(arrived[:, local_subjects:], axis=0)
    reduced = jnp.concatenate([jnp.stack(group_parts), velocity_chunk])
    copies = jnp.broadcast_to(reduced[None], (peers,) + reduced.shape)
    gathered = lax.all_to_all(copies, "subj", 0, 0, tiled=True).transpose(1, 0, 2)
    template_sum = gathered[:groups].reshape(templates.shape)
    new_templates = template_sum / denominator
    velocity = gathered[groups:].reshape(3, slab_depth, slab_rows, cell_count)
    return (new_templates, velocity)


def solution(mesh):
    in_specs = (P("subj", "gz", "gy", None), P(None, "gz", "gy", None), P(), P())
    out_specs = (P(None, "gz", "gy", None), P(None, "gz", "gy", None))
    return jax.shard_map(local, mesh=mesh, in_specs=in_specs, out_specs=out_specs, check_vma=False)
```

```python
from functools import partial
from functools import reduce

import jax
import jax.numpy as jnp
from jax import lax
from jax.sharding import PartitionSpec as P

BOX_EPS = 1e-05
SPREAD = (0.0625, 0.25, 0.375, 0.25, 0.0625)
REACH = 4
SPILL = 2


def rim(x, side, dim, width):
    length = x.shape[dim]
    if side < 0:
        return lax.slice_in_dim(x, length - width, length, axis=dim)
    if side > 0:
        return lax.slice_in_dim(x, 0, width, axis=dim)
    return x


def halo_exchange(x, width):
    nz, ny = (lax.axis_size("gz"), lax.axis_size("gy"))
    grid = {}
    for sz in (-1, 0, 1):
        for sy in (-1, 0, 1):
            if sz == 0 and sy == 0:
                grid[sz, sy] = x
                continue
            piece = rim(rim(x, sz, 1, width), sy, 2, width)
            perm = []
            for gz in range(nz):
                for gy in range(ny):
                    tz, ty = (gz - sz, gy - sy)
                    if 0 <= tz < nz and 0 <= ty < ny:
                        perm.append((gz * ny + gy, tz * ny + ty))
            grid[sz, sy] = lax.ppermute(piece, ("gz", "gy"), perm)
    bands = [
        jnp.concatenate([grid[sz, -1], grid[sz, 0], grid[sz, 1]], axis=2) for sz in (-1, 0, 1)
    ]
    return jnp.concatenate(bands, axis=1)


def add_pair(former, latter):
    return former + latter


def window_sum(volume, along_axis, length, extent):
    inner = volume.shape[along_axis] - 2
    triple = reduce(
        add_pair,
        [lax.slice_in_dim(volume, offset, offset + inner, axis=along_axis) for offset in range(3)],
    )
    pieces = [
        lax.slice_in_dim(triple, offset, offset + length, axis=along_axis)
        for offset in range(0, extent, 3)
    ]
    return reduce(add_pair, pieces)


def weighted(volume, along_axis, length):
    pieces = [
        SPREAD[offset] * lax.slice_in_dim(volume, offset, offset + length, axis=along_axis)
        for offset in range(5)
    ]
    return reduce(add_pair, pieces)


def box_local(padded, slab_depth, slab_rows):
    widened = jnp.pad(padded, ((0, 0), (0, 0), (4, 4)))
    along_x = window_sum(widened, 2, padded.shape[2], 9)
    along_y = window_sum(along_x, 1, slab_rows, 9)
    return window_sum(along_y, 0, slab_depth, 9)


def smooth_local(padded, slab_depth, slab_rows):
    widened = jnp.pad(padded, ((0, 0), (0, 0), (2, 2)))
    along_x = weighted(widened, 2, padded.shape[2])
    along_y = weighted(along_x, 1, slab_rows)
    return weighted(along_y, 0, slab_depth)


def template_stats(templ_pad, slab_depth, slab_rows):
    templ_mean = box_local(templ_pad, slab_depth, slab_rows) / 729.0
    templ_var = (
        box_local(templ_pad * templ_pad, slab_depth, slab_rows) / 729.0
        - templ_mean * templ_mean
        + BOX_EPS
    )
    return (templ_mean, templ_var)


def region_masks(extents, z_index, y_index):
    inside_z = (z_index[None, :] >= extents[:, 0:1]) & (z_index[None, :] < extents[:, 1:2])
    inside_y = (y_index[None, :] >= extents[:, 2:3]) & (y_index[None, :] < extents[:, 3:4])
    return (inside_z[:, :, None] & inside_y[:, None, :]).astype(jnp.float32)


def subject_force(image_pad, templ_pad, region_mask, in_grid, slab_depth, slab_rows):
    templ_mean, templ_var = template_stats(templ_pad, slab_depth, slab_rows)
    mean_i = box_local(image_pad, slab_depth, slab_rows) / 729.0
    square_mean = box_local(image_pad * image_pad, slab_depth, slab_rows) / 729.0
    cross_mean = box_local(image_pad * templ_pad, slab_depth, slab_rows) / 729.0
    var_i = square_mean - mean_i * mean_i + BOX_EPS
    covariance = cross_mean - mean_i * templ_mean
    image_mid = image_pad[4 : 4 + slab_depth, 4 : 4 + slab_rows, :]
    templ_mid = templ_pad[4 : 4 + slab_depth, 4 : 4 + slab_rows, :]
    centred_i = image_mid - mean_i
    centred_t = templ_mid - templ_mean
    factor = (
        region_mask
        * (2.0 * covariance / (var_i * templ_var))
        * (centred_t - covariance / var_i * centred_i)
    )
    grad_z = 0.5 * (
        image_pad[5 : 5 + slab_depth, 4 : 4 + slab_rows, :]
        - image_pad[3 : 3 + slab_depth, 4 : 4 + slab_rows, :]
    )
    grad_y = 0.5 * (
        image_pad[4 : 4 + slab_depth, 5 : 5 + slab_rows, :]
        - image_pad[4 : 4 + slab_depth, 3 : 3 + slab_rows, :]
    )
    side_pad = jnp.pad(image_mid, ((0, 0), (0, 0), (1, 1)))
    grad_x = 0.5 * (side_pad[:, :, 2:] - side_pad[:, :, :-2])
    force = jnp.stack([factor * grad_z, factor * grad_y, factor * grad_x])
    return jnp.where(in_grid[None], force, 0.0)


def local(subjects, templates, group_of, extents):
    local_subjects, slab_depth, slab_rows, cell_count = subjects.shape
    groups = templates.shape[0]
    peers = lax.axis_size("subj")
    cells = slab_depth * slab_rows * cell_count
    chunk = cells // peers
    depth_out, rows_out = (slab_depth + 2 * SPILL, slab_rows + 2 * SPILL)
    total_z, total_y = (slab_depth * lax.axis_size("gz"), slab_rows * lax.axis_size("gy"))
    first_subject = lax.axis_index("subj") * local_subjects
    own_groups = lax.dynamic_slice_in_dim(group_of, first_subject, local_subjects)
    own_templates = jnp.take(templates, own_groups, axis=0)
    z_start = lax.axis_index("gz") * slab_depth
    y_start = lax.axis_index("gy") * slab_rows
    z_index = z_start + jnp.arange(slab_depth, dtype=jnp.int32)
    y_index = y_start + jnp.arange(slab_rows, dtype=jnp.int32)
    all_masks = region_masks(extents, z_index, y_index)
    own_masks = lax.dynamic_slice_in_dim(all_masks, first_subject, local_subjects)
    onehot = (group_of[:, None] == jnp.arange(groups, dtype=jnp.int32)[None, :]).astype(jnp.float32)
    counts = jnp.sum(onehot[:, :, None, None] * all_masks[:, None], axis=0)
    denominator = jnp.maximum(counts, 1.0)[..., None]

    z_wide = z_start - SPILL + jnp.arange(depth_out, dtype=jnp.int32)
    y_wide = y_start - SPILL + jnp.arange(rows_out, dtype=jnp.int32)
    wide_masks = lax.dynamic_slice_in_dim(
        region_masks(extents, z_wide, y_wide), first_subject, local_subjects
    )
    in_grid = (
        ((z_wide >= 0) & (z_wide < total_z))[:, None, None]
        & ((y_wide >= 0) & (y_wide < total_y))[None, :, None]
    )

    masked = own_masks[..., None] * subjects
    outgoing = masked.reshape(local_subjects, peers, chunk).transpose(1, 0, 2)
    arrived = lax.all_to_all(outgoing, "subj", 0, 0, tiled=True)
    images = arrived.reshape(peers * local_subjects, chunk)
    group_parts = jnp.stack(
        [jnp.sum(jnp.where((group_of == g)[:, None], images, 0.0), axis=0) for g in range(groups)]
    )
    copies = jnp.broadcast_to(group_parts[None], (peers,) + group_parts.shape)
    gathered = lax.all_to_all(copies, "subj", 0, 0, tiled=True).transpose(1, 0, 2)

    volumes = jnp.concatenate([own_templates, subjects], axis=0)
    padded = halo_exchange(volumes, REACH + SPILL)
    gathered, padded = lax.optimization_barrier((gathered, padded))
    new_templates = gathered.reshape(templates.shape) / denominator
    templ_all = padded[:local_subjects]
    image_all = padded[local_subjects:]
    forces = jax.vmap(
        partial(subject_force, in_grid=in_grid, slab_depth=depth_out, slab_rows=rows_out)
    )(image_all, templ_all, wide_masks[..., None])
    force_sum = jnp.sum(forces, axis=0)
    smoother = jax.vmap(partial(smooth_local, slab_depth=slab_depth, slab_rows=slab_rows))
    velocity_part = smoother(force_sum)

    outgoing = velocity_part.reshape(3, peers, chunk).transpose(1, 0, 2)
    velocity_chunk = jnp.sum(lax.all_to_all(outgoing, "subj", 0, 0, tiled=True), axis=0)
    copies = jnp.broadcast_to(velocity_chunk[None], (peers,) + velocity_chunk.shape)
    gathered = lax.all_to_all(copies, "subj", 0, 0, tiled=True).transpose(1, 0, 2)
    velocity = gathered.reshape(3, slab_depth, slab_rows, cell_count)
    return (new_templates, velocity)


def solution(mesh):
    in_specs = (P("subj", "gz", "gy", None), P(None, "gz", "gy", None), P(), P())
    out_specs = (P(None, "gz", "gy", None), P(None, "gz", "gy", None))
    return jax.shard_map(local, mesh=mesh, in_specs=in_specs, out_specs=out_specs, check_vma=False)
```

```python
from functools import partial
from functools import reduce

import jax
import jax.numpy as jnp
from jax import lax
from jax.sharding import PartitionSpec as P

BOX_EPS = 1e-05
SPREAD = (0.0625, 0.25, 0.375, 0.25, 0.0625)
REACH = 4
SPILL = 2


def rim(x, side, dim, width):
    length = x.shape[dim]
    if side < 0:
        return lax.slice_in_dim(x, length - width, length, axis=dim)
    if side > 0:
        return lax.slice_in_dim(x, 0, width, axis=dim)
    return x


def halo_exchange(x, width):
    nz, ny = (lax.axis_size("gz"), lax.axis_size("gy"))
    grid = {}
    for sz in (-1, 0, 1):
        for sy in (-1, 0, 1):
            if sz == 0 and sy == 0:
                grid[sz, sy] = x
                continue
            piece = rim(rim(x, sz, 1, width), sy, 2, width)
            perm = []
            for gz in range(nz):
                for gy in range(ny):
                    tz, ty = (gz - sz, gy - sy)
                    if 0 <= tz < nz and 0 <= ty < ny:
                        perm.append((gz * ny + gy, tz * ny + ty))
            grid[sz, sy] = lax.ppermute(piece, ("gz", "gy"), perm)
    bands = [
        jnp.concatenate([grid[sz, -1], grid[sz, 0], grid[sz, 1]], axis=2) for sz in (-1, 0, 1)
    ]
    return jnp.concatenate(bands, axis=1)


def add_pair(former, latter):
    return former + latter


def window_sum(volume, along_axis, length, extent):
    inner = volume.shape[along_axis] - 2
    triple = reduce(
        add_pair,
        [lax.slice_in_dim(volume, offset, offset + inner, axis=along_axis) for offset in range(3)],
    )
    pieces = [
        lax.slice_in_dim(triple, offset, offset + length, axis=along_axis)
        for offset in range(0, extent, 3)
    ]
    return reduce(add_pair, pieces)


def weighted(volume, along_axis, length):
    pieces = [
        SPREAD[offset] * lax.slice_in_dim(volume, offset, offset + length, axis=along_axis)
        for offset in range(5)
    ]
    return reduce(add_pair, pieces)


def box_local(padded, slab_depth, slab_rows):
    widened = jnp.pad(padded, ((0, 0), (0, 0), (4, 4)))
    along_x = window_sum(widened, 2, padded.shape[2], 9)
    along_y = window_sum(along_x, 1, slab_rows, 9)
    return window_sum(along_y, 0, slab_depth, 9)


def smooth_local(padded, slab_depth, slab_rows):
    widened = jnp.pad(padded, ((0, 0), (0, 0), (2, 2)))
    along_x = weighted(widened, 2, padded.shape[2])
    along_y = weighted(along_x, 1, slab_rows)
    return weighted(along_y, 0, slab_depth)


def template_stats(templ_pad, slab_depth, slab_rows):
    templ_mean = box_local(templ_pad, slab_depth, slab_rows) / 729.0
    templ_var = (
        box_local(templ_pad * templ_pad, slab_depth, slab_rows) / 729.0
        - templ_mean * templ_mean
        + BOX_EPS
    )
    return (templ_mean, templ_var)


def region_masks(extents, z_index, y_index):
    inside_z = (z_index[None, :] >= extents[:, 0:1]) & (z_index[None, :] < extents[:, 1:2])
    inside_y = (y_index[None, :] >= extents[:, 2:3]) & (y_index[None, :] < extents[:, 3:4])
    return (inside_z[:, :, None] & inside_y[:, None, :]).astype(jnp.float32)


def subject_force(image_pad, templ_pad, region_mask, in_grid, slab_depth, slab_rows):
    templ_mean, templ_var = template_stats(templ_pad, slab_depth, slab_rows)
    mean_i = box_local(image_pad, slab_depth, slab_rows) / 729.0
    square_mean = box_local(image_pad * image_pad, slab_depth, slab_rows) / 729.0
    cross_mean = box_local(image_pad * templ_pad, slab_depth, slab_rows) / 729.0
    var_i = square_mean - mean_i * mean_i + BOX_EPS
    covariance = cross_mean - mean_i * templ_mean
    image_mid = image_pad[4 : 4 + slab_depth, 4 : 4 + slab_rows, :]
    templ_mid = templ_pad[4 : 4 + slab_depth, 4 : 4 + slab_rows, :]
    centred_i = image_mid - mean_i
    centred_t = templ_mid - templ_mean
    factor = (
        region_mask
        * (2.0 * covariance / (var_i * templ_var))
        * (centred_t - covariance / var_i * centred_i)
    )
    grad_z = 0.5 * (
        image_pad[5 : 5 + slab_depth, 4 : 4 + slab_rows, :]
        - image_pad[3 : 3 + slab_depth, 4 : 4 + slab_rows, :]
    )
    grad_y = 0.5 * (
        image_pad[4 : 4 + slab_depth, 5 : 5 + slab_rows, :]
        - image_pad[4 : 4 + slab_depth, 3 : 3 + slab_rows, :]
    )
    side_pad = jnp.pad(image_mid, ((0, 0), (0, 0), (1, 1)))
    grad_x = 0.5 * (side_pad[:, :, 2:] - side_pad[:, :, :-2])
    force = jnp.stack([factor * grad_z, factor * grad_y, factor * grad_x])
    return jnp.where(in_grid[None], force, 0.0)


def local(subjects, templates, group_of, extents):
    local_subjects, slab_depth, slab_rows, cell_count = subjects.shape
    groups = templates.shape[0]
    peers = lax.axis_size("subj")
    cells = slab_depth * slab_rows * cell_count
    chunk = cells // peers
    depth_out, rows_out = (slab_depth + 2 * SPILL, slab_rows + 2 * SPILL)
    total_z, total_y = (slab_depth * lax.axis_size("gz"), slab_rows * lax.axis_size("gy"))
    first_subject = lax.axis_index("subj") * local_subjects
    own_groups = lax.dynamic_slice_in_dim(group_of, first_subject, local_subjects)
    own_templates = jnp.take(templates, own_groups, axis=0)
    z_start = lax.axis_index("gz") * slab_depth
    y_start = lax.axis_index("gy") * slab_rows
    z_index = z_start + jnp.arange(slab_depth, dtype=jnp.int32)
    y_index = y_start + jnp.arange(slab_rows, dtype=jnp.int32)
    all_masks = region_masks(extents, z_index, y_index)
    own_masks = lax.dynamic_slice_in_dim(all_masks, first_subject, local_subjects)
    onehot = (group_of[:, None] == jnp.arange(groups, dtype=jnp.int32)[None, :]).astype(jnp.float32)
    counts = jnp.sum(onehot[:, :, None, None] * all_masks[:, None], axis=0)
    denominator = jnp.maximum(counts, 1.0)[..., None]

    z_wide = z_start - SPILL + jnp.arange(depth_out, dtype=jnp.int32)
    y_wide = y_start - SPILL + jnp.arange(rows_out, dtype=jnp.int32)
    wide_masks = lax.dynamic_slice_in_dim(
        region_masks(extents, z_wide, y_wide), first_subject, local_subjects
    )
    in_grid = (
        ((z_wide >= 0) & (z_wide < total_z))[:, None, None]
        & ((y_wide >= 0) & (y_wide < total_y))[None, :, None]
    )

    volumes = jnp.concatenate([own_templates, subjects], axis=0)
    padded = halo_exchange(volumes, REACH + SPILL)
    templ_all = padded[:local_subjects]
    image_all = padded[local_subjects:]
    forces = jax.vmap(
        partial(subject_force, in_grid=in_grid, slab_depth=depth_out, slab_rows=rows_out)
    )(image_all, templ_all, wide_masks[..., None])
    force_sum = jnp.sum(forces, axis=0)
    smoother = jax.vmap(partial(smooth_local, slab_depth=slab_depth, slab_rows=slab_rows))
    velocity_part = smoother(force_sum)

    masked = own_masks[..., None] * subjects
    outgoing = jnp.concatenate(
        [masked.reshape(local_subjects, peers, chunk), velocity_part.reshape(3, peers, chunk)]
    ).transpose(1, 0, 2)
    arrived = lax.all_to_all(outgoing, "subj", 0, 0, tiled=True)
    images = arrived[:, :local_subjects].reshape(peers * local_subjects, chunk)
    group_parts = [
        jnp.sum(jnp.where((group_of == g)[:, None], images, 0.0), axis=0) for g in range(groups)
    ]
    velocity_chunk = jnp.sum(arrived[:, local_subjects:], axis=0)
    reduced = jnp.concatenate([jnp.stack(group_parts), velocity_chunk])
    copies = jnp.broadcast_to(reduced[None], (peers,) + reduced.shape)
    gathered = lax.all_to_all(copies, "subj", 0, 0, tiled=True).transpose(1, 0, 2)
    template_sum = gathered[:groups].reshape(templates.shape)
    new_templates = template_sum / denominator
    velocity = gathered[groups:].reshape(3, slab_depth, slab_rows, cell_count)
    return (new_templates, velocity)


def solution(mesh):
    in_specs = (P("subj", "gz", "gy", None), P(None, "gz", "gy", None), P(), P())
    out_specs = (P(None, "gz", "gy", None), P(None, "gz", "gy", None))
    return jax.shard_map(local, mesh=mesh, in_specs=in_specs, out_specs=out_specs, check_vma=False)
```

```python
from functools import partial
from functools import reduce

import jax
import jax.numpy as jnp
from jax import lax
from jax.sharding import PartitionSpec as P

BOX_EPS = 1e-05
SPREAD = (0.0625, 0.25, 0.375, 0.25, 0.0625)
REACH = 4
SPILL = 2


def rim(x, side, dim, width):
    length = x.shape[dim]
    if side < 0:
        return lax.slice_in_dim(x, length - width, length, axis=dim)
    if side > 0:
        return lax.slice_in_dim(x, 0, width, axis=dim)
    return x


def halo_exchange(x, width):
    nz, ny = (lax.axis_size("gz"), lax.axis_size("gy"))
    grid = {}
    for sz in (-1, 0, 1):
        for sy in (-1, 0, 1):
            if sz == 0 and sy == 0:
                grid[sz, sy] = x
                continue
            piece = rim(rim(x, sz, 1, width), sy, 2, width)
            perm = []
            for gz in range(nz):
                for gy in range(ny):
                    tz, ty = (gz - sz, gy - sy)
                    if 0 <= tz < nz and 0 <= ty < ny:
                        perm.append((gz * ny + gy, tz * ny + ty))
            grid[sz, sy] = lax.ppermute(piece, ("gz", "gy"), perm)
    bands = [
        jnp.concatenate([grid[sz, -1], grid[sz, 0], grid[sz, 1]], axis=2) for sz in (-1, 0, 1)
    ]
    return jnp.concatenate(bands, axis=1)


def add_pair(former, latter):
    return former + latter


def window_sum(volume, along_axis, length, extent):
    inner = volume.shape[along_axis] - 2
    triple = reduce(
        add_pair,
        [lax.slice_in_dim(volume, offset, offset + inner, axis=along_axis) for offset in range(3)],
    )
    pieces = [
        lax.slice_in_dim(triple, offset, offset + length, axis=along_axis)
        for offset in range(0, extent, 3)
    ]
    return reduce(add_pair, pieces)


def weighted(volume, along_axis, length):
    pieces = [
        SPREAD[offset] * lax.slice_in_dim(volume, offset, offset + length, axis=along_axis)
        for offset in range(5)
    ]
    return reduce(add_pair, pieces)


def box_local(padded, slab_depth, slab_rows):
    widened = jnp.pad(padded, ((0, 0), (0, 0), (4, 4)))
    along_x = window_sum(widened, 2, padded.shape[2], 9)
    along_y = window_sum(along_x, 1, slab_rows, 9)
    return window_sum(along_y, 0, slab_depth, 9)


def smooth_local(padded, slab_depth, slab_rows):
    widened = jnp.pad(padded, ((0, 0), (0, 0), (2, 2)))
    along_x = weighted(widened, 2, padded.shape[2])
    along_y = weighted(along_x, 1, slab_rows)
    return weighted(along_y, 0, slab_depth)


def template_stats(templ_pad, slab_depth, slab_rows):
    templ_mean = box_local(templ_pad, slab_depth, slab_rows) / 729.0
    templ_var = (
        box_local(templ_pad * templ_pad, slab_depth, slab_rows) / 729.0
        - templ_mean * templ_mean
        + BOX_EPS
    )
    return (templ_mean, templ_var)


def region_masks(extents, z_index, y_index):
    inside_z = (z_index[None, :] >= extents[:, 0:1]) & (z_index[None, :] < extents[:, 1:2])
    inside_y = (y_index[None, :] >= extents[:, 2:3]) & (y_index[None, :] < extents[:, 3:4])
    return (inside_z[:, :, None] & inside_y[:, None, :]).astype(jnp.float32)


def subject_force(image_pad, templ_pad, region_mask, in_grid, slab_depth, slab_rows):
    templ_mean, templ_var = template_stats(templ_pad, slab_depth, slab_rows)
    mean_i = box_local(image_pad, slab_depth, slab_rows) / 729.0
    square_mean = box_local(image_pad * image_pad, slab_depth, slab_rows) / 729.0
    cross_mean = box_local(image_pad * templ_pad, slab_depth, slab_rows) / 729.0
    var_i = square_mean - mean_i * mean_i + BOX_EPS
    covariance = cross_mean - mean_i * templ_mean
    image_mid = image_pad[4 : 4 + slab_depth, 4 : 4 + slab_rows, :]
    templ_mid = templ_pad[4 : 4 + slab_depth, 4 : 4 + slab_rows, :]
    centred_i = image_mid - mean_i
    centred_t = templ_mid - templ_mean
    factor = (
        region_mask
        * (2.0 * covariance / (var_i * templ_var))
        * (centred_t - covariance / var_i * centred_i)
    )
    grad_z = 0.5 * (
        image_pad[5 : 5 + slab_depth, 4 : 4 + slab_rows, :]
        - image_pad[3 : 3 + slab_depth, 4 : 4 + slab_rows, :]
    )
    grad_y = 0.5 * (
        image_pad[4 : 4 + slab_depth, 5 : 5 + slab_rows, :]
        - image_pad[4 : 4 + slab_depth, 3 : 3 + slab_rows, :]
    )
    side_pad = jnp.pad(image_mid, ((0, 0), (0, 0), (1, 1)))
    grad_x = 0.5 * (side_pad[:, :, 2:] - side_pad[:, :, :-2])
    force = jnp.stack([factor * grad_z, factor * grad_y, factor * grad_x])
    return jnp.where(in_grid[None], force, 0.0)


def step(subjects, templates, group_of, extents):
    local_subjects, slab_depth, slab_rows, cell_count = subjects.shape
    groups = templates.shape[0]
    peers = lax.axis_size("subj")
    cells = slab_depth * slab_rows * cell_count
    chunk = cells // peers
    depth_out, rows_out = (slab_depth + 2 * SPILL, slab_rows + 2 * SPILL)
    total_z, total_y = (slab_depth * lax.axis_size("gz"), slab_rows * lax.axis_size("gy"))
    first_subject = lax.axis_index("subj") * local_subjects
    own_groups = lax.dynamic_slice_in_dim(group_of, first_subject, local_subjects)
    own_templates = jnp.take(templates, own_groups, axis=0)
    z_start = lax.axis_index("gz") * slab_depth
    y_start = lax.axis_index("gy") * slab_rows
    z_index = z_start + jnp.arange(slab_depth, dtype=jnp.int32)
    y_index = y_start + jnp.arange(slab_rows, dtype=jnp.int32)
    all_masks = region_masks(extents, z_index, y_index)
    own_masks = lax.dynamic_slice_in_dim(all_masks, first_subject, local_subjects)
    onehot = (group_of[:, None] == jnp.arange(groups, dtype=jnp.int32)[None, :]).astype(jnp.float32)
    counts = jnp.sum(onehot[:, :, None, None] * all_masks[:, None], axis=0)
    denominator = jnp.maximum(counts, 1.0)[..., None]

    z_wide = z_start - SPILL + jnp.arange(depth_out, dtype=jnp.int32)
    y_wide = y_start - SPILL + jnp.arange(rows_out, dtype=jnp.int32)
    wide_masks = lax.dynamic_slice_in_dim(
        region_masks(extents, z_wide, y_wide), first_subject, local_subjects
    )
    in_grid = (
        ((z_wide >= 0) & (z_wide < total_z))[:, None, None]
        & ((y_wide >= 0) & (y_wide < total_y))[None, :, None]
    )

    masked = (own_masks[..., None] * subjects).reshape(local_subjects, peers, chunk)
    arrived = lax.all_to_all(masked, "subj", 1, 1, tiled=True)
    images = arrived.transpose(1, 0, 2).reshape(peers * local_subjects, chunk)
    group_parts = jnp.stack(
        [jnp.sum(jnp.where((group_of == g)[:, None], images, 0.0), axis=0) for g in range(groups)]
    )
    copies = jnp.broadcast_to(group_parts[:, None], (groups, peers, chunk))
    gathered = lax.all_to_all(copies, "subj", 1, 1, tiled=True)

    volumes = jnp.concatenate([own_templates, subjects], axis=0)
    padded = halo_exchange(volumes, REACH + SPILL)
    gathered, padded = lax.optimization_barrier((gathered, padded))
    new_templates = gathered.reshape(templates.shape) / denominator
    templ_all = padded[:local_subjects]
    image_all = padded[local_subjects:]
    forces = jax.vmap(
        partial(subject_force, in_grid=in_grid, slab_depth=depth_out, slab_rows=rows_out)
    )(image_all, templ_all, wide_masks[..., None])
    force_sum = jnp.sum(forces, axis=0)
    smoother = jax.vmap(partial(smooth_local, slab_depth=slab_depth, slab_rows=slab_rows))
    velocity_part = smoother(force_sum).reshape(3, peers, chunk)

    velocity_chunk = jnp.sum(lax.all_to_all(velocity_part, "subj", 1, 1, tiled=True), axis=1)
    copies = jnp.broadcast_to(velocity_chunk[:, None], (3, peers, chunk))
    gathered = lax.all_to_all(copies, "subj", 1, 1, tiled=True)
    velocity = gathered.reshape(3, slab_depth, slab_rows, cell_count)
    return (new_templates, velocity)


def solution(mesh):
    in_specs = (P("subj", "gz", "gy", None), P(None, "gz", "gy", None), P(), P())
    out_specs = (P(None, "gz", "gy", None), P(None, "gz", "gy", None))
    return jax.shard_map(step, mesh=mesh, in_specs=in_specs, out_specs=out_specs, check_vma=False)
```

```python
from functools import partial
from functools import reduce

import jax
import jax.numpy as jnp
from jax import lax
from jax.sharding import PartitionSpec as P

BOX_EPS = 1e-05
SPREAD = (0.0625, 0.25, 0.375, 0.25, 0.0625)
REACH = 4
SPILL = 2


def rim(x, side, dim, width):
    length = x.shape[dim]
    if side < 0:
        return lax.slice_in_dim(x, length - width, length, axis=dim)
    if side > 0:
        return lax.slice_in_dim(x, 0, width, axis=dim)
    return x


def halo_exchange(x, width):
    nz, ny = (lax.axis_size("gz"), lax.axis_size("gy"))
    grid = {}
    for sz in (-1, 0, 1):
        for sy in (-1, 0, 1):
            if sz == 0 and sy == 0:
                grid[sz, sy] = x
                continue
            piece = rim(rim(x, sz, 1, width), sy, 2, width)
            perm = []
            for gz in range(nz):
                for gy in range(ny):
                    tz, ty = (gz - sz, gy - sy)
                    if 0 <= tz < nz and 0 <= ty < ny:
                        perm.append((gz * ny + gy, tz * ny + ty))
            grid[sz, sy] = lax.ppermute(piece, ("gz", "gy"), perm)
    bands = [
        jnp.concatenate([grid[sz, -1], grid[sz, 0], grid[sz, 1]], axis=2) for sz in (-1, 0, 1)
    ]
    return jnp.concatenate(bands, axis=1)


def add_pair(former, latter):
    return former + latter


def window_sum(volume, along_axis, length, extent):
    inner = volume.shape[along_axis] - 2
    triple = reduce(
        add_pair,
        [lax.slice_in_dim(volume, offset, offset + inner, axis=along_axis) for offset in range(3)],
    )
    pieces = [
        lax.slice_in_dim(triple, offset, offset + length, axis=along_axis)
        for offset in range(0, extent, 3)
    ]
    return reduce(add_pair, pieces)


def weighted(volume, along_axis, length):
    pieces = [
        SPREAD[offset] * lax.slice_in_dim(volume, offset, offset + length, axis=along_axis)
        for offset in range(5)
    ]
    return reduce(add_pair, pieces)


def box_local(padded, slab_depth, slab_rows):
    along_z = window_sum(padded, 0, slab_depth, 9)
    along_y = window_sum(along_z, 1, slab_rows, 9)
    widened = jnp.pad(along_y, ((0, 0), (0, 0), (4, 4)))
    return window_sum(widened, 2, padded.shape[2], 9)


def smooth_local(padded, slab_depth, slab_rows):
    along_z = weighted(padded, 0, slab_depth)
    along_y = weighted(along_z, 1, slab_rows)
    widened = jnp.pad(along_y, ((0, 0), (0, 0), (2, 2)))
    return weighted(widened, 2, padded.shape[2])


def template_stats(templ_pad, slab_depth, slab_rows):
    templ_mean = box_local(templ_pad, slab_depth, slab_rows) / 729.0
    templ_var = (
        box_local(templ_pad * templ_pad, slab_depth, slab_rows) / 729.0
        - templ_mean * templ_mean
        + BOX_EPS
    )
    return (templ_mean, templ_var)


def region_masks(extents, z_index, y_index):
    inside_z = (z_index[None, :] >= extents[:, 0:1]) & (z_index[None, :] < extents[:, 1:2])
    inside_y = (y_index[None, :] >= extents[:, 2:3]) & (y_index[None, :] < extents[:, 3:4])
    return (inside_z[:, :, None] & inside_y[:, None, :]).astype(jnp.float32)


def subject_force(image_pad, templ_pad, region_mask, in_grid, slab_depth, slab_rows):
    templ_mean, templ_var = template_stats(templ_pad, slab_depth, slab_rows)
    mean_i = box_local(image_pad, slab_depth, slab_rows) / 729.0
    square_mean = box_local(image_pad * image_pad, slab_depth, slab_rows) / 729.0
    cross_mean = box_local(image_pad * templ_pad, slab_depth, slab_rows) / 729.0
    var_i = square_mean - mean_i * mean_i + BOX_EPS
    covariance = cross_mean - mean_i * templ_mean
    image_mid = image_pad[4 : 4 + slab_depth, 4 : 4 + slab_rows, :]
    templ_mid = templ_pad[4 : 4 + slab_depth, 4 : 4 + slab_rows, :]
    centred_i = image_mid - mean_i
    centred_t = templ_mid - templ_mean
    factor = (
        region_mask
        * (2.0 * covariance / (var_i * templ_var))
        * (centred_t - covariance / var_i * centred_i)
    )
    grad_z = 0.5 * (
        image_pad[5 : 5 + slab_depth, 4 : 4 + slab_rows, :]
        - image_pad[3 : 3 + slab_depth, 4 : 4 + slab_rows, :]
    )
    grad_y = 0.5 * (
        image_pad[4 : 4 + slab_depth, 5 : 5 + slab_rows, :]
        - image_pad[4 : 4 + slab_depth, 3 : 3 + slab_rows, :]
    )
    side_pad = jnp.pad(image_mid, ((0, 0), (0, 0), (1, 1)))
    grad_x = 0.5 * (side_pad[:, :, 2:] - side_pad[:, :, :-2])
    force = jnp.stack([factor * grad_z, factor * grad_y, factor * grad_x])
    return jnp.where(in_grid[None], force, 0.0)


def local(subjects, templates, group_of, extents):
    local_subjects, slab_depth, slab_rows, cell_count = subjects.shape
    groups = templates.shape[0]
    peers = lax.axis_size("subj")
    cells = slab_depth * slab_rows * cell_count
    chunk = cells // peers
    depth_out, rows_out = (slab_depth + 2 * SPILL, slab_rows + 2 * SPILL)
    total_z, total_y = (slab_depth * lax.axis_size("gz"), slab_rows * lax.axis_size("gy"))
    first_subject = lax.axis_index("subj") * local_subjects
    own_groups = lax.dynamic_slice_in_dim(group_of, first_subject, local_subjects)
    own_templates = jnp.take(templates, own_groups, axis=0)
    z_start = lax.axis_index("gz") * slab_depth
    y_start = lax.axis_index("gy") * slab_rows
    z_index = z_start + jnp.arange(slab_depth, dtype=jnp.int32)
    y_index = y_start + jnp.arange(slab_rows, dtype=jnp.int32)
    all_masks = region_masks(extents, z_index, y_index)
    own_masks = lax.dynamic_slice_in_dim(all_masks, first_subject, local_subjects)
    onehot = (group_of[:, None] == jnp.arange(groups, dtype=jnp.int32)[None, :]).astype(jnp.float32)
    counts = jnp.sum(onehot[:, :, None, None] * all_masks[:, None], axis=0)
    denominator = jnp.maximum(counts, 1.0)[..., None]

    z_wide = z_start - SPILL + jnp.arange(depth_out, dtype=jnp.int32)
    y_wide = y_start - SPILL + jnp.arange(rows_out, dtype=jnp.int32)
    wide_masks = lax.dynamic_slice_in_dim(
        region_masks(extents, z_wide, y_wide), first_subject, local_subjects
    )
    in_grid = (
        ((z_wide >= 0) & (z_wide < total_z))[:, None, None]
        & ((y_wide >= 0) & (y_wide < total_y))[None, :, None]
    )

    volumes = jnp.concatenate([own_templates, subjects], axis=0)
    padded = halo_exchange(volumes, REACH + SPILL)
    templ_all = padded[:local_subjects]
    image_all = padded[local_subjects:]
    forces = jax.vmap(
        partial(subject_force, in_grid=in_grid, slab_depth=depth_out, slab_rows=rows_out)
    )(image_all, templ_all, wide_masks[..., None])
    force_sum = jnp.sum(forces, axis=0)
    smoother = jax.vmap(partial(smooth_local, slab_depth=slab_depth, slab_rows=slab_rows))
    velocity_part = smoother(force_sum)

    masked = own_masks[..., None] * subjects
    outgoing = jnp.concatenate(
        [masked.reshape(local_subjects, peers, chunk), velocity_part.reshape(3, peers, chunk)]
    ).transpose(1, 0, 2)
    arrived = lax.all_to_all(outgoing, "subj", 0, 0, tiled=True)
    images = arrived[:, :local_subjects].reshape(peers * local_subjects, chunk)
    group_parts = [
        jnp.sum(jnp.where((group_of == g)[:, None], images, 0.0), axis=0) for g in range(groups)
    ]
    velocity_chunk = jnp.sum(arrived[:, local_subjects:], axis=0)
    reduced = jnp.concatenate([jnp.stack(group_parts), velocity_chunk])
    copies = jnp.broadcast_to(reduced[None], (peers,) + reduced.shape)
    gathered = lax.all_to_all(copies, "subj", 0, 0, tiled=True).transpose(1, 0, 2)
    template_sum = gathered[:groups].reshape(templates.shape)
    new_templates = template_sum / denominator
    velocity = gathered[groups:].reshape(3, slab_depth, slab_rows, cell_count)
    return (new_templates, velocity)


def solution(mesh):
    in_specs = (P("subj", "gz", "gy", None), P(None, "gz", "gy", None), P(), P())
    out_specs = (P(None, "gz", "gy", None), P(None, "gz", "gy", None))
    return jax.shard_map(local, mesh=mesh, in_specs=in_specs, out_specs=out_specs, check_vma=False)
```

```python
from functools import partial
from functools import reduce

import jax
import jax.numpy as jnp
from jax import lax
from jax.sharding import PartitionSpec as P

BOX_EPS = 1e-05
SPREAD = (0.0625, 0.25, 0.375, 0.25, 0.0625)
REACH = 4
SPILL = 2


def rim(x, side, dim, width):
    length = x.shape[dim]
    if side < 0:
        return lax.slice_in_dim(x, length - width, length, axis=dim)
    if side > 0:
        return lax.slice_in_dim(x, 0, width, axis=dim)
    return x


def halo_exchange(x, width):
    for axis, dim in (("gz", 1), ("gy", 2)):
        peers = lax.axis_size(axis)
        up = [(i, i + 1) for i in range(peers - 1)]
        down = [(j, i) for i, j in up]
        before = lax.ppermute(rim(x, -1, dim, width), axis, up)
        after = lax.ppermute(rim(x, 1, dim, width), axis, down)
        x = jnp.concatenate([before, x, after], axis=dim)
    return x


def add_pair(former, latter):
    return former + latter


def window_sum(volume, along_axis, length, extent):
    inner = volume.shape[along_axis] - 2
    triple = reduce(
        add_pair,
        [lax.slice_in_dim(volume, offset, offset + inner, axis=along_axis) for offset in range(3)],
    )
    pieces = [
        lax.slice_in_dim(triple, offset, offset + length, axis=along_axis)
        for offset in range(0, extent, 3)
    ]
    return reduce(add_pair, pieces)


def weighted(volume, along_axis, length):
    pieces = [
        SPREAD[offset] * lax.slice_in_dim(volume, offset, offset + length, axis=along_axis)
        for offset in range(5)
    ]
    return reduce(add_pair, pieces)


def box_local(padded, slab_depth, slab_rows):
    along_z = window_sum(padded, 0, slab_depth, 9)
    along_y = window_sum(along_z, 1, slab_rows, 9)
    widened = jnp.pad(along_y, ((0, 0), (0, 0), (4, 4)))
    return window_sum(widened, 2, padded.shape[2], 9)


def smooth_local(padded, slab_depth, slab_rows):
    along_z = weighted(padded, 0, slab_depth)
    along_y = weighted(along_z, 1, slab_rows)
    widened = jnp.pad(along_y, ((0, 0), (0, 0), (2, 2)))
    return weighted(widened, 2, padded.shape[2])


def template_stats(templ_pad, slab_depth, slab_rows):
    templ_mean = box_local(templ_pad, slab_depth, slab_rows) / 729.0
    templ_var = (
        box_local(templ_pad * templ_pad, slab_depth, slab_rows) / 729.0
        - templ_mean * templ_mean
        + BOX_EPS
    )
    return (templ_mean, templ_var)


def region_masks(extents, z_index, y_index):
    inside_z = (z_index[None, :] >= extents[:, 0:1]) & (z_index[None, :] < extents[:, 1:2])
    inside_y = (y_index[None, :] >= extents[:, 2:3]) & (y_index[None, :] < extents[:, 3:4])
    return (inside_z[:, :, None] & inside_y[:, None, :]).astype(jnp.float32)


def subject_force(image_pad, templ_pad, region_mask, in_grid, slab_depth, slab_rows):
    templ_mean, templ_var = template_stats(templ_pad, slab_depth, slab_rows)
    mean_i = box_local(image_pad, slab_depth, slab_rows) / 729.0
    square_mean = box_local(image_pad * image_pad, slab_depth, slab_rows) / 729.0
    cross_mean = box_local(image_pad * templ_pad, slab_depth, slab_rows) / 729.0
    var_i = square_mean - mean_i * mean_i + BOX_EPS
    covariance = cross_mean - mean_i * templ_mean
    image_mid = image_pad[4 : 4 + slab_depth, 4 : 4 + slab_rows, :]
    templ_mid = templ_pad[4 : 4 + slab_depth, 4 : 4 + slab_rows, :]
    centred_i = image_mid - mean_i
    centred_t = templ_mid - templ_mean
    factor = (
        region_mask
        * (2.0 * covariance / (var_i * templ_var))
        * (centred_t - covariance / var_i * centred_i)
    )
    grad_z = 0.5 * (
        image_pad[5 : 5 + slab_depth, 4 : 4 + slab_rows, :]
        - image_pad[3 : 3 + slab_depth, 4 : 4 + slab_rows, :]
    )
    grad_y = 0.5 * (
        image_pad[4 : 4 + slab_depth, 5 : 5 + slab_rows, :]
        - image_pad[4 : 4 + slab_depth, 3 : 3 + slab_rows, :]
    )
    side_pad = jnp.pad(image_mid, ((0, 0), (0, 0), (1, 1)))
    grad_x = 0.5 * (side_pad[:, :, 2:] - side_pad[:, :, :-2])
    force = jnp.stack([factor * grad_z, factor * grad_y, factor * grad_x])
    return jnp.where(in_grid[None], force, 0.0)


def local(subjects, templates, group_of, extents):
    local_subjects, slab_depth, slab_rows, cell_count = subjects.shape
    groups = templates.shape[0]
    peers = lax.axis_size("subj")
    cells = slab_depth * slab_rows * cell_count
    chunk = cells // peers
    depth_out, rows_out = (slab_depth + 2 * SPILL, slab_rows + 2 * SPILL)
    total_z, total_y = (slab_depth * lax.axis_size("gz"), slab_rows * lax.axis_size("gy"))
    first_subject = lax.axis_index("subj") * local_subjects
    own_groups = lax.dynamic_slice_in_dim(group_of, first_subject, local_subjects)
    own_templates = jnp.take(templates, own_groups, axis=0)
    z_start = lax.axis_index("gz") * slab_depth
    y_start = lax.axis_index("gy") * slab_rows
    z_index = z_start + jnp.arange(slab_depth, dtype=jnp.int32)
    y_index = y_start + jnp.arange(slab_rows, dtype=jnp.int32)
    all_masks = region_masks(extents, z_index, y_index)
    own_masks = lax.dynamic_slice_in_dim(all_masks, first_subject, local_subjects)
    onehot = (group_of[:, None] == jnp.arange(groups, dtype=jnp.int32)[None, :]).astype(jnp.float32)
    counts = jnp.sum(onehot[:, :, None, None] * all_masks[:, None], axis=0)
    denominator = jnp.maximum(counts, 1.0)[..., None]

    z_wide = z_start - SPILL + jnp.arange(depth_out, dtype=jnp.int32)
    y_wide = y_start - SPILL + jnp.arange(rows_out, dtype=jnp.int32)
    wide_masks = lax.dynamic_slice_in_dim(
        region_masks(extents, z_wide, y_wide), first_subject, local_subjects
    )
    in_grid = (
        ((z_wide >= 0) & (z_wide < total_z))[:, None, None]
        & ((y_wide >= 0) & (y_wide < total_y))[None, :, None]
    )

    volumes = jnp.concatenate([own_templates, subjects], axis=0)
    padded = halo_exchange(volumes, REACH + SPILL)
    templ_all = padded[:local_subjects]
    image_all = padded[local_subjects:]
    forces = jax.vmap(
        partial(subject_force, in_grid=in_grid, slab_depth=depth_out, slab_rows=rows_out)
    )(image_all, templ_all, wide_masks[..., None])
    force_sum = jnp.sum(forces, axis=0)
    smoother = jax.vmap(partial(smooth_local, slab_depth=slab_depth, slab_rows=slab_rows))
    velocity_part = smoother(force_sum)

    masked = own_masks[..., None] * subjects
    outgoing = jnp.concatenate(
        [masked.reshape(local_subjects, peers, chunk), velocity_part.reshape(3, peers, chunk)]
    ).transpose(1, 0, 2)
    arrived = lax.all_to_all(outgoing, "subj", 0, 0, tiled=True)
    images = arrived[:, :local_subjects].reshape(peers * local_subjects, chunk)
    group_parts = [
        jnp.sum(jnp.where((group_of == g)[:, None], images, 0.0), axis=0) for g in range(groups)
    ]
    velocity_chunk = jnp.sum(arrived[:, local_subjects:], axis=0)
    reduced = jnp.concatenate([jnp.stack(group_parts), velocity_chunk])
    copies = jnp.broadcast_to(reduced[None], (peers,) + reduced.shape)
    gathered = lax.all_to_all(copies, "subj", 0, 0, tiled=True).transpose(1, 0, 2)
    template_sum = gathered[:groups].reshape(templates.shape)
    new_templates = template_sum / denominator
    velocity = gathered[groups:].reshape(3, slab_depth, slab_rows, cell_count)
    return (new_templates, velocity)


def solution(mesh):
    in_specs = (P("subj", "gz", "gy", None), P(None, "gz", "gy", None), P(), P())
    out_specs = (P(None, "gz", "gy", None), P(None, "gz", "gy", None))
    return jax.shard_map(local, mesh=mesh, in_specs=in_specs, out_specs=out_specs, check_vma=False)
```

```python
from functools import partial
from functools import reduce

import jax
import jax.numpy as jnp
from jax import lax
from jax.sharding import PartitionSpec as P

BOX_EPS = 1e-05
SPREAD = (0.0625, 0.25, 0.375, 0.25, 0.0625)
REACH = 4
SPILL = 2


def rim(x, side, dim, width):
    length = x.shape[dim]
    if side < 0:
        return lax.slice_in_dim(x, length - width, length, axis=dim)
    if side > 0:
        return lax.slice_in_dim(x, 0, width, axis=dim)
    return x


def halo_exchange(x, width):
    nz, ny = (lax.axis_size("gz"), lax.axis_size("gy"))
    grid = {(0, 0): x}
    sides = [(-1, 0), (1, 0), (-1, -1), (-1, 1), (1, -1), (1, 1), (0, -1), (0, 1)]
    for sz, sy in sides:
        piece = rim(rim(x, sz, 1, width), sy, 2, width)
        perm = []
        for gz in range(nz):
            for gy in range(ny):
                tz, ty = (gz - sz, gy - sy)
                if 0 <= tz < nz and 0 <= ty < ny:
                    perm.append((gz * ny + gy, tz * ny + ty))
        grid[sz, sy] = lax.ppermute(piece, ("gz", "gy"), perm)
    shape = list(x.shape)
    shape[1] += 2 * width
    shape[2] += 2 * width
    padded = jnp.zeros(shape, x.dtype)
    for sz, sy in [(0, 0)] + sides:
        z_at = {-1: 0, 0: width, 1: width + x.shape[1]}[sz]
        y_at = {-1: 0, 0: width, 1: width + x.shape[2]}[sy]
        padded = lax.dynamic_update_slice(padded, grid[sz, sy], (0, z_at, y_at, 0))
    return padded


def add_pair(former, latter):
    return former + latter


def window_sum(volume, along_axis, length, extent):
    inner = volume.shape[along_axis] - 2
    triple = reduce(
        add_pair,
        [lax.slice_in_dim(volume, offset, offset + inner, axis=along_axis) for offset in range(3)],
    )
    pieces = [
        lax.slice_in_dim(triple, offset, offset + length, axis=along_axis)
        for offset in range(0, extent, 3)
    ]
    return reduce(add_pair, pieces)


def weighted(volume, along_axis, length):
    pieces = [
        SPREAD[offset] * lax.slice_in_dim(volume, offset, offset + length, axis=along_axis)
        for offset in range(5)
    ]
    return reduce(add_pair, pieces)


def box_local(padded, slab_depth, slab_rows):
    along_z = window_sum(padded, 0, slab_depth, 9)
    along_y = window_sum(along_z, 1, slab_rows, 9)
    widened = jnp.pad(along_y, ((0, 0), (0, 0), (4, 4)))
    return window_sum(widened, 2, padded.shape[2], 9)


def smooth_local(padded, slab_depth, slab_rows):
    along_z = weighted(padded, 0, slab_depth)
    along_y = weighted(along_z, 1, slab_rows)
    widened = jnp.pad(along_y, ((0, 0), (0, 0), (2, 2)))
    return weighted(widened, 2, padded.shape[2])


def template_stats(templ_pad, slab_depth, slab_rows):
    templ_mean = box_local(templ_pad, slab_depth, slab_rows) / 729.0
    templ_var = (
        box_local(templ_pad * templ_pad, slab_depth, slab_rows) / 729.0
        - templ_mean * templ_mean
        + BOX_EPS
    )
    return (templ_mean, templ_var)


def region_masks(extents, z_index, y_index):
    inside_z = (z_index[None, :] >= extents[:, 0:1]) & (z_index[None, :] < extents[:, 1:2])
    inside_y = (y_index[None, :] >= extents[:, 2:3]) & (y_index[None, :] < extents[:, 3:4])
    return (inside_z[:, :, None] & inside_y[:, None, :]).astype(jnp.float32)


def subject_force(image_pad, templ_pad, region_mask, in_grid, slab_depth, slab_rows):
    templ_mean, templ_var = template_stats(templ_pad, slab_depth, slab_rows)
    mean_i = box_local(image_pad, slab_depth, slab_rows) / 729.0
    square_mean = box_local(image_pad * image_pad, slab_depth, slab_rows) / 729.0
    cross_mean = box_local(image_pad * templ_pad, slab_depth, slab_rows) / 729.0
    var_i = square_mean - mean_i * mean_i + BOX_EPS
    covariance = cross_mean - mean_i * templ_mean
    image_mid = image_pad[4 : 4 + slab_depth, 4 : 4 + slab_rows, :]
    templ_mid = templ_pad[4 : 4 + slab_depth, 4 : 4 + slab_rows, :]
    centred_i = image_mid - mean_i
    centred_t = templ_mid - templ_mean
    factor = (
        region_mask
        * (2.0 * covariance / (var_i * templ_var))
        * (centred_t - covariance / var_i * centred_i)
    )
    grad_z = 0.5 * (
        image_pad[5 : 5 + slab_depth, 4 : 4 + slab_rows, :]
        - image_pad[3 : 3 + slab_depth, 4 : 4 + slab_rows, :]
    )
    grad_y = 0.5 * (
        image_pad[4 : 4 + slab_depth, 5 : 5 + slab_rows, :]
        - image_pad[4 : 4 + slab_depth, 3 : 3 + slab_rows, :]
    )
    side_pad = jnp.pad(image_mid, ((0, 0), (0, 0), (1, 1)))
    grad_x = 0.5 * (side_pad[:, :, 2:] - side_pad[:, :, :-2])
    force = jnp.stack([factor * grad_z, factor * grad_y, factor * grad_x])
    return jnp.where(in_grid[None], force, 0.0)


def local(subjects, templates, group_of, extents):
    local_subjects, slab_depth, slab_rows, cell_count = subjects.shape
    groups = templates.shape[0]
    peers = lax.axis_size("subj")
    cells = slab_depth * slab_rows * cell_count
    chunk = cells // peers
    depth_out, rows_out = (slab_depth + 2 * SPILL, slab_rows + 2 * SPILL)
    total_z, total_y = (slab_depth * lax.axis_size("gz"), slab_rows * lax.axis_size("gy"))
    first_subject = lax.axis_index("subj") * local_subjects
    own_groups = lax.dynamic_slice_in_dim(group_of, first_subject, local_subjects)
    own_templates = jnp.take(templates, own_groups, axis=0)
    z_start = lax.axis_index("gz") * slab_depth
    y_start = lax.axis_index("gy") * slab_rows
    z_index = z_start + jnp.arange(slab_depth, dtype=jnp.int32)
    y_index = y_start + jnp.arange(slab_rows, dtype=jnp.int32)
    all_masks = region_masks(extents, z_index, y_index)
    own_masks = lax.dynamic_slice_in_dim(all_masks, first_subject, local_subjects)
    onehot = (group_of[:, None] == jnp.arange(groups, dtype=jnp.int32)[None, :]).astype(jnp.float32)
    counts = jnp.sum(onehot[:, :, None, None] * all_masks[:, None], axis=0)
    denominator = jnp.maximum(counts, 1.0)[..., None]

    z_wide = z_start - SPILL + jnp.arange(depth_out, dtype=jnp.int32)
    y_wide = y_start - SPILL + jnp.arange(rows_out, dtype=jnp.int32)
    wide_masks = lax.dynamic_slice_in_dim(
        region_masks(extents, z_wide, y_wide), first_subject, local_subjects
    )
    in_grid = (
        ((z_wide >= 0) & (z_wide < total_z))[:, None, None]
        & ((y_wide >= 0) & (y_wide < total_y))[None, :, None]
    )

    volumes = jnp.concatenate([own_templates, subjects], axis=0)
    padded = halo_exchange(volumes, REACH + SPILL)
    templ_all = padded[:local_subjects]
    image_all = padded[local_subjects:]
    forces = jax.vmap(
        partial(subject_force, in_grid=in_grid, slab_depth=depth_out, slab_rows=rows_out)
    )(image_all, templ_all, wide_masks[..., None])
    force_sum = jnp.sum(forces, axis=0)
    smoother = jax.vmap(partial(smooth_local, slab_depth=slab_depth, slab_rows=slab_rows))
    velocity_part = smoother(force_sum)

    masked = own_masks[..., None] * subjects
    outgoing = jnp.concatenate(
        [masked.reshape(local_subjects, peers, chunk), velocity_part.reshape(3, peers, chunk)]
    ).transpose(1, 0, 2)
    arrived = lax.all_to_all(outgoing, "subj", 0, 0, tiled=True)
    images = arrived[:, :local_subjects].reshape(peers * local_subjects, chunk)
    group_parts = [
        jnp.sum(jnp.where((group_of == g)[:, None], images, 0.0), axis=0) for g in range(groups)
    ]
    velocity_chunk = jnp.sum(arrived[:, local_subjects:], axis=0)
    own_chunk = lax.axis_index("subj") * chunk
    spread = jnp.broadcast_to(denominator, templates.shape).reshape(groups, cells)
    chunk_denominator = lax.dynamic_slice_in_dim(spread, own_chunk, chunk, axis=1)
    reduced = jnp.concatenate([jnp.stack(group_parts) / chunk_denominator, velocity_chunk])
    copies = jnp.broadcast_to(reduced[None], (peers,) + reduced.shape)
    gathered = lax.all_to_all(copies, "subj", 0, 0, tiled=True).transpose(1, 0, 2)
    template_sum = gathered[:groups].reshape(templates.shape)
    new_templates = template_sum
    velocity = gathered[groups:].reshape(3, slab_depth, slab_rows, cell_count)
    return (new_templates, velocity)


def solution(mesh):
    in_specs = (P("subj", "gz", "gy", None), P(None, "gz", "gy", None), P(), P())
    out_specs = (P(None, "gz", "gy", None), P(None, "gz", "gy", None))
    return jax.shard_map(local, mesh=mesh, in_specs=in_specs, out_specs=out_specs, check_vma=False)
```

```python
from functools import partial
from functools import reduce

import jax
import jax.numpy as jnp
from jax import lax
from jax.sharding import PartitionSpec as P

BOX_EPS = 1e-05
SPREAD = (0.0625, 0.25, 0.375, 0.25, 0.0625)
REACH = 4
SPILL = 2


def rim(x, side, dim, width):
    length = x.shape[dim]
    if side < 0:
        return lax.slice_in_dim(x, length - width, length, axis=dim)
    if side > 0:
        return lax.slice_in_dim(x, 0, width, axis=dim)
    return x


def halo_exchange(x, width):
    nz, ny = (lax.axis_size("gz"), lax.axis_size("gy"))
    grid = {}
    for sz in (-1, 0, 1):
        for sy in (-1, 0, 1):
            if sz == 0 and sy == 0:
                grid[sz, sy] = x
                continue
            piece = rim(rim(x, sz, 1, width), sy, 2, width)
            perm = []
            for gz in range(nz):
                for gy in range(ny):
                    tz, ty = (gz - sz, gy - sy)
                    if 0 <= tz < nz and 0 <= ty < ny:
                        perm.append((gz * ny + gy, tz * ny + ty))
            grid[sz, sy] = lax.ppermute(piece, ("gz", "gy"), perm)
    bands = [
        jnp.concatenate([grid[sz, -1], grid[sz, 0], grid[sz, 1]], axis=2) for sz in (-1, 0, 1)
    ]
    return jnp.concatenate(bands, axis=1)


def add_pair(former, latter):
    return former + latter


def window_sum(volume, along_axis, length, extent):
    inner = volume.shape[along_axis] - 2
    triple = reduce(
        add_pair,
        [lax.slice_in_dim(volume, offset, offset + inner, axis=along_axis) for offset in range(3)],
    )
    pieces = [
        lax.slice_in_dim(triple, offset, offset + length, axis=along_axis)
        for offset in range(0, extent, 3)
    ]
    return reduce(add_pair, pieces)


def weighted(volume, along_axis, length):
    pieces = [
        SPREAD[offset] * lax.slice_in_dim(volume, offset, offset + length, axis=along_axis)
        for offset in range(5)
    ]
    return reduce(add_pair, pieces)


def box_local(padded, slab_depth, slab_rows):
    along_z = window_sum(padded, 0, slab_depth, 9)
    along_y = window_sum(along_z, 1, slab_rows, 9)
    widened = jnp.pad(along_y, ((0, 0), (0, 0), (4, 4)))
    return window_sum(widened, 2, padded.shape[2], 9)


def smooth_local(padded, slab_depth, slab_rows):
    along_z = weighted(padded, 0, slab_depth)
    along_y = weighted(along_z, 1, slab_rows)
    widened = jnp.pad(along_y, ((0, 0), (0, 0), (2, 2)))
    return weighted(widened, 2, padded.shape[2])


def template_stats(templ_pad, slab_depth, slab_rows):
    templ_mean = box_local(templ_pad, slab_depth, slab_rows) / 729.0
    templ_var = (
        box_local(templ_pad * templ_pad, slab_depth, slab_rows) / 729.0
        - templ_mean * templ_mean
        + BOX_EPS
    )
    return (templ_mean, templ_var)


def region_masks(extents, z_index, y_index):
    inside_z = (z_index[None, :] >= extents[:, 0:1]) & (z_index[None, :] < extents[:, 1:2])
    inside_y = (y_index[None, :] >= extents[:, 2:3]) & (y_index[None, :] < extents[:, 3:4])
    return (inside_z[:, :, None] & inside_y[:, None, :]).astype(jnp.float32)


def subject_force(image_pad, templ_pad, region_mask, in_grid, slab_depth, slab_rows):
    templ_mean, templ_var = template_stats(templ_pad, slab_depth, slab_rows)
    mean_i = box_local(image_pad, slab_depth, slab_rows) / 729.0
    square_mean = box_local(image_pad * image_pad, slab_depth, slab_rows) / 729.0
    cross_mean = box_local(image_pad * templ_pad, slab_depth, slab_rows) / 729.0
    var_i = square_mean - mean_i * mean_i + BOX_EPS
    covariance = cross_mean - mean_i * templ_mean
    image_mid = image_pad[4 : 4 + slab_depth, 4 : 4 + slab_rows, :]
    templ_mid = templ_pad[4 : 4 + slab_depth, 4 : 4 + slab_rows, :]
    centred_i = image_mid - mean_i
    centred_t = templ_mid - templ_mean
    factor = (
        region_mask
        * (2.0 * covariance / (var_i * templ_var))
        * (centred_t - covariance / var_i * centred_i)
    )
    grad_z = 0.5 * (
        image_pad[5 : 5 + slab_depth, 4 : 4 + slab_rows, :]
        - image_pad[3 : 3 + slab_depth, 4 : 4 + slab_rows, :]
    )
    grad_y = 0.5 * (
        image_pad[4 : 4 + slab_depth, 5 : 5 + slab_rows, :]
        - image_pad[4 : 4 + slab_depth, 3 : 3 + slab_rows, :]
    )
    side_pad = jnp.pad(image_mid, ((0, 0), (0, 0), (1, 1)))
    grad_x = 0.5 * (side_pad[:, :, 2:] - side_pad[:, :, :-2])
    force = jnp.stack([factor * grad_z, factor * grad_y, factor * grad_x])
    return jnp.where(in_grid[None], force, 0.0)


def local(subjects, templates, group_of, extents):
    local_subjects, slab_depth, slab_rows, cell_count = subjects.shape
    groups = templates.shape[0]
    peers = lax.axis_size("subj")
    cells = slab_depth * slab_rows * cell_count
    chunk = cells // peers
    depth_out, rows_out = (slab_depth + 2 * SPILL, slab_rows + 2 * SPILL)
    total_z, total_y = (slab_depth * lax.axis_size("gz"), slab_rows * lax.axis_size("gy"))
    first_subject = lax.axis_index("subj") * local_subjects
    own_groups = lax.dynamic_slice_in_dim(group_of, first_subject, local_subjects)
    own_templates = jnp.concatenate(
        [lax.dynamic_slice_in_dim(templates, own_groups[l], 1) for l in range(local_subjects)]
    )
    z_start = lax.axis_index("gz") * slab_depth
    y_start = lax.axis_index("gy") * slab_rows
    z_index = z_start + jnp.arange(slab_depth, dtype=jnp.int32)
    y_index = y_start + jnp.arange(slab_rows, dtype=jnp.int32)
    all_masks = region_masks(extents, z_index, y_index)
    own_masks = lax.dynamic_slice_in_dim(all_masks, first_subject, local_subjects)
    onehot = (group_of[:, None] == jnp.arange(groups, dtype=jnp.int32)[None, :]).astype(jnp.float32)
    counts = jnp.sum(onehot[:, :, None, None] * all_masks[:, None], axis=0)
    denominator = jnp.maximum(counts, 1.0)[..., None]

    z_wide = z_start - SPILL + jnp.arange(depth_out, dtype=jnp.int32)
    y_wide = y_start - SPILL + jnp.arange(rows_out, dtype=jnp.int32)
    wide_masks = lax.dynamic_slice_in_dim(
        region_masks(extents, z_wide, y_wide), first_subject, local_subjects
    )
    in_grid = (
        ((z_wide >= 0) & (z_wide < total_z))[:, None, None]
        & ((y_wide >= 0) & (y_wide < total_y))[None, :, None]
    )

    volumes = jnp.concatenate([own_templates, subjects], axis=0)
    padded = halo_exchange(volumes, REACH + SPILL)
    templ_all = padded[:local_subjects]
    image_all = padded[local_subjects:]
    forces = jax.vmap(
        partial(subject_force, in_grid=in_grid, slab_depth=depth_out, slab_rows=rows_out)
    )(image_all, templ_all, wide_masks[..., None])
    force_sum = jnp.sum(forces, axis=0)
    smoother = jax.vmap(partial(smooth_local, slab_depth=slab_depth, slab_rows=slab_rows))
    velocity_part = smoother(force_sum)

    masked = own_masks[..., None] * subjects
    outgoing = jnp.concatenate(
        [masked.reshape(local_subjects, peers, chunk), velocity_part.reshape(3, peers, chunk)]
    ).transpose(1, 0, 2)
    arrived = lax.all_to_all(outgoing, "subj", 0, 0, tiled=True)
    images = arrived[:, :local_subjects].reshape(peers * local_subjects, chunk)
    group_parts = [
        jnp.sum(jnp.where((group_of == g)[:, None], images, 0.0), axis=0) for g in range(groups)
    ]
    velocity_chunk = jnp.sum(arrived[:, local_subjects:], axis=0)
    reduced = jnp.concatenate([jnp.stack(group_parts), velocity_chunk])
    lanes = 128 if reduced.size % 128 == 0 else reduced.shape[-1]
    flat = reduced.reshape(-1, lanes)
    copies = jnp.broadcast_to(flat[None], (peers,) + flat.shape)
    gathered = lax.all_to_all(copies, "subj", 0, 0, tiled=True)
    gathered = gathered.reshape((peers,) + reduced.shape).transpose(1, 0, 2)
    template_sum = gathered[:groups].reshape(templates.shape)
    new_templates = template_sum / denominator
    velocity = gathered[groups:].reshape(3, slab_depth, slab_rows, cell_count)
    return (new_templates, velocity)


def solution(mesh):
    in_specs = (P("subj", "gz", "gy", None), P(None, "gz", "gy", None), P(), P())
    out_specs = (P(None, "gz", "gy", None), P(None, "gz", "gy", None))
    return jax.shard_map(local, mesh=mesh, in_specs=in_specs, out_specs=out_specs, check_vma=False)
```

```python
from functools import partial
from functools import reduce

import jax
import jax.numpy as jnp
from jax import lax
from jax.sharding import PartitionSpec as P

BOX_EPS = 1e-05
SPREAD = (0.0625, 0.25, 0.375, 0.25, 0.0625)
REACH = 4
SPILL = 2


def rim(x, side, dim, width):
    length = x.shape[dim]
    if side < 0:
        return lax.slice_in_dim(x, length - width, length, axis=dim)
    if side > 0:
        return lax.slice_in_dim(x, 0, width, axis=dim)
    return x


def halo_exchange(x, width):
    nz, ny = (lax.axis_size("gz"), lax.axis_size("gy"))
    grid = {}
    for sz in (-1, 0, 1):
        for sy in (-1, 0, 1):
            if sz == 0 and sy == 0:
                grid[sz, sy] = x
                continue
            piece = rim(rim(x, sz, 1, width), sy, 2, width)
            perm = []
            for gz in range(nz):
                for gy in range(ny):
                    tz, ty = (gz - sz, gy - sy)
                    if 0 <= tz < nz and 0 <= ty < ny:
                        perm.append((gz * ny + gy, tz * ny + ty))
            grid[sz, sy] = lax.ppermute(piece, ("gz", "gy"), perm)
    bands = [
        jnp.concatenate([grid[sz, -1], grid[sz, 0], grid[sz, 1]], axis=2) for sz in (-1, 0, 1)
    ]
    return jnp.concatenate(bands, axis=1)


def add_pair(former, latter):
    return former + latter


def window_sum(volume, along_axis, length, extent):
    inner = volume.shape[along_axis] - 2
    triple = reduce(
        add_pair,
        [lax.slice_in_dim(volume, offset, offset + inner, axis=along_axis) for offset in range(3)],
    )
    pieces = [
        lax.slice_in_dim(triple, offset, offset + length, axis=along_axis)
        for offset in range(0, extent, 3)
    ]
    return reduce(add_pair, pieces)


def weighted(volume, along_axis, length):
    pieces = [
        SPREAD[offset] * lax.slice_in_dim(volume, offset, offset + length, axis=along_axis)
        for offset in range(5)
    ]
    return reduce(add_pair, pieces)


def box_local(padded, slab_depth, slab_rows):
    along_z = window_sum(padded, 0, slab_depth, 9)
    along_y = window_sum(along_z, 1, slab_rows, 9)
    widened = jnp.pad(along_y, ((0, 0), (0, 0), (4, 4)))
    return window_sum(widened, 2, padded.shape[2], 9)


def smooth_local(padded, slab_depth, slab_rows):
    along_z = weighted(padded, 0, slab_depth)
    along_y = weighted(along_z, 1, slab_rows)
    widened = jnp.pad(along_y, ((0, 0), (0, 0), (2, 2)))
    return weighted(widened, 2, padded.shape[2])


def template_stats(templ_pad, slab_depth, slab_rows):
    templ_mean = box_local(templ_pad, slab_depth, slab_rows) / 729.0
    templ_var = (
        box_local(templ_pad * templ_pad, slab_depth, slab_rows) / 729.0
        - templ_mean * templ_mean
        + BOX_EPS
    )
    return (templ_mean, templ_var)


def region_masks(extents, z_index, y_index):
    inside_z = (z_index[None, :] >= extents[:, 0:1]) & (z_index[None, :] < extents[:, 1:2])
    inside_y = (y_index[None, :] >= extents[:, 2:3]) & (y_index[None, :] < extents[:, 3:4])
    return (inside_z[:, :, None] & inside_y[:, None, :]).astype(jnp.float32)


def subject_force(image_pad, templ_pad, region_mask, in_grid, slab_depth, slab_rows):
    templ_mean, templ_var = template_stats(templ_pad, slab_depth, slab_rows)
    mean_i = box_local(image_pad, slab_depth, slab_rows) / 729.0
    square_mean = box_local(image_pad * image_pad, slab_depth, slab_rows) / 729.0
    cross_mean = box_local(image_pad * templ_pad, slab_depth, slab_rows) / 729.0
    var_i = square_mean - mean_i * mean_i + BOX_EPS
    covariance = cross_mean - mean_i * templ_mean
    image_mid = image_pad[4 : 4 + slab_depth, 4 : 4 + slab_rows, :]
    templ_mid = templ_pad[4 : 4 + slab_depth, 4 : 4 + slab_rows, :]
    centred_i = image_mid - mean_i
    centred_t = templ_mid - templ_mean
    factor = (
        region_mask
        * (2.0 * covariance / (var_i * templ_var))
        * (centred_t - covariance / var_i * centred_i)
    )
    grad_z = 0.5 * (
        image_pad[5 : 5 + slab_depth, 4 : 4 + slab_rows, :]
        - image_pad[3 : 3 + slab_depth, 4 : 4 + slab_rows, :]
    )
    grad_y = 0.5 * (
        image_pad[4 : 4 + slab_depth, 5 : 5 + slab_rows, :]
        - image_pad[4 : 4 + slab_depth, 3 : 3 + slab_rows, :]
    )
    side_pad = jnp.pad(image_mid, ((0, 0), (0, 0), (1, 1)))
    grad_x = 0.5 * (side_pad[:, :, 2:] - side_pad[:, :, :-2])
    force = jnp.stack([factor * grad_z, factor * grad_y, factor * grad_x])
    return jnp.where(in_grid[None], force, 0.0)


def local(subjects, templates, group_of, extents):
    local_subjects, slab_depth, slab_rows, cell_count = subjects.shape
    groups = templates.shape[0]
    peers = lax.axis_size("subj")
    cells = slab_depth * slab_rows * cell_count
    chunk = cells // peers
    depth_out, rows_out = (slab_depth + 2 * SPILL, slab_rows + 2 * SPILL)
    total_z, total_y = (slab_depth * lax.axis_size("gz"), slab_rows * lax.axis_size("gy"))
    first_subject = lax.axis_index("subj") * local_subjects
    own_groups = lax.dynamic_slice_in_dim(group_of, first_subject, local_subjects)
    own_templates = jnp.broadcast_to(templates[0], subjects.shape)
    for g in range(1, groups):
        own_templates = jnp.where(
            (own_groups == g)[:, None, None, None], templates[g][None], own_templates
        )
    z_start = lax.axis_index("gz") * slab_depth
    y_start = lax.axis_index("gy") * slab_rows
    z_index = z_start + jnp.arange(slab_depth, dtype=jnp.int32)
    y_index = y_start + jnp.arange(slab_rows, dtype=jnp.int32)
    all_masks = region_masks(extents, z_index, y_index)
    own_masks = lax.dynamic_slice_in_dim(all_masks, first_subject, local_subjects)
    onehot = (group_of[:, None] == jnp.arange(groups, dtype=jnp.int32)[None, :]).astype(jnp.float32)
    counts = jnp.sum(onehot[:, :, None, None] * all_masks[:, None], axis=0)
    denominator = jnp.maximum(counts, 1.0)[..., None]

    z_wide = z_start - SPILL + jnp.arange(depth_out, dtype=jnp.int32)
    y_wide = y_start - SPILL + jnp.arange(rows_out, dtype=jnp.int32)
    wide_masks = lax.dynamic_slice_in_dim(
        region_masks(extents, z_wide, y_wide), first_subject, local_subjects
    )
    in_grid = (
        ((z_wide >= 0) & (z_wide < total_z))[:, None, None]
        & ((y_wide >= 0) & (y_wide < total_y))[None, :, None]
    )

    volumes = jnp.concatenate([own_templates, subjects], axis=0)
    padded = halo_exchange(volumes, REACH + SPILL)
    templ_all = padded[:local_subjects]
    image_all = padded[local_subjects:]
    forces = jax.vmap(
        partial(subject_force, in_grid=in_grid, slab_depth=depth_out, slab_rows=rows_out)
    )(image_all, templ_all, wide_masks[..., None])
    force_sum = jnp.sum(forces, axis=0)
    smoother = jax.vmap(partial(smooth_local, slab_depth=slab_depth, slab_rows=slab_rows))
    velocity_part = smoother(force_sum)

    masked = own_masks[..., None] * subjects
    outgoing = jnp.concatenate(
        [masked.reshape(local_subjects, peers, chunk), velocity_part.reshape(3, peers, chunk)]
    ).transpose(1, 0, 2)
    arrived = lax.all_to_all(outgoing, "subj", 0, 0, tiled=True)
    images = arrived[:, :local_subjects].reshape(peers * local_subjects, chunk)
    group_parts = [
        jnp.sum(jnp.where((group_of == g)[:, None], images, 0.0), axis=0) for g in range(groups)
    ]
    velocity_chunk = jnp.sum(arrived[:, local_subjects:], axis=0)
    own_chunk = lax.axis_index("subj") * chunk
    spread = jnp.broadcast_to(denominator, templates.shape).reshape(groups, cells)
    chunk_denominator = lax.dynamic_slice_in_dim(spread, own_chunk, chunk, axis=1)
    reduced = jnp.concatenate([jnp.stack(group_parts) / chunk_denominator, velocity_chunk])
    lanes = 128 if reduced.size % 128 == 0 else reduced.shape[-1]
    flat = reduced.reshape(-1, lanes)
    copies = jnp.broadcast_to(flat[None], (peers,) + flat.shape)
    gathered = lax.all_to_all(copies, "subj", 0, 0, tiled=True)
    gathered = gathered.reshape((peers,) + reduced.shape).transpose(1, 0, 2)
    template_sum = gathered[:groups].reshape(templates.shape)
    new_templates = template_sum
    velocity = gathered[groups:].reshape(3, slab_depth, slab_rows, cell_count)
    return (new_templates, velocity)


def solution(mesh):
    in_specs = (P("subj", "gz", "gy", None), P(None, "gz", "gy", None), P(), P())
    out_specs = (P(None, "gz", "gy", None), P(None, "gz", "gy", None))
    return jax.shard_map(local, mesh=mesh, in_specs=in_specs, out_specs=out_specs, check_vma=False)
```

```python
from functools import partial
from functools import reduce

import jax
import jax.numpy as jnp
from jax import lax
from jax.sharding import PartitionSpec as P

BOX_EPS = 1e-05
SPREAD = (0.0625, 0.25, 0.375, 0.25, 0.0625)
REACH = 4
SPILL = 2


def rim(x, side, dim, width):
    length = x.shape[dim]
    if side < 0:
        return lax.slice_in_dim(x, length - width, length, axis=dim)
    if side > 0:
        return lax.slice_in_dim(x, 0, width, axis=dim)
    return x


def halo_exchange(x, width):
    nz, ny = (lax.axis_size("gz"), lax.axis_size("gy"))
    grid = {}
    for sz in (-1, 0, 1):
        for sy in (-1, 0, 1):
            if sz == 0 and sy == 0:
                grid[sz, sy] = x
                continue
            piece = rim(rim(x, sz, 1, width), sy, 2, width)
            perm = []
            for gz in range(nz):
                for gy in range(ny):
                    tz, ty = (gz - sz, gy - sy)
                    if 0 <= tz < nz and 0 <= ty < ny:
                        perm.append((gz * ny + gy, tz * ny + ty))
            grid[sz, sy] = lax.ppermute(piece, ("gz", "gy"), perm)
    bands = [
        jnp.concatenate([grid[sz, -1], grid[sz, 0], grid[sz, 1]], axis=2) for sz in (-1, 0, 1)
    ]
    return jnp.concatenate(bands, axis=1)


def add_pair(former, latter):
    return former + latter


def window_sum(volume, along_axis, length, extent):
    inner = volume.shape[along_axis] - 2
    triple = reduce(
        add_pair,
        [lax.slice_in_dim(volume, offset, offset + inner, axis=along_axis) for offset in range(3)],
    )
    pieces = [
        lax.slice_in_dim(triple, offset, offset + length, axis=along_axis)
        for offset in range(0, extent, 3)
    ]
    return reduce(add_pair, pieces)


def weighted(volume, along_axis, length):
    pieces = [
        SPREAD[offset] * lax.slice_in_dim(volume, offset, offset + length, axis=along_axis)
        for offset in range(5)
    ]
    return reduce(add_pair, pieces)


def box_local(padded, slab_depth, slab_rows):
    along_z = window_sum(padded, 0, slab_depth, 9)
    along_y = window_sum(along_z, 1, slab_rows, 9)
    widened = jnp.pad(along_y, ((0, 0), (0, 0), (4, 4)))
    return window_sum(widened, 2, padded.shape[2], 9)


def smooth_local(padded, slab_depth, slab_rows):
    along_z = weighted(padded, 0, slab_depth)
    along_y = weighted(along_z, 1, slab_rows)
    widened = jnp.pad(along_y, ((0, 0), (0, 0), (2, 2)))
    return weighted(widened, 2, padded.shape[2])


def template_stats(templ_pad, slab_depth, slab_rows):
    templ_mean = box_local(templ_pad, slab_depth, slab_rows) / 729.0
    templ_var = (
        box_local(templ_pad * templ_pad, slab_depth, slab_rows) / 729.0
        - templ_mean * templ_mean
        + BOX_EPS
    )
    return (templ_mean, templ_var)


def region_masks(extents, z_index, y_index):
    inside_z = (z_index[None, :] >= extents[:, 0:1]) & (z_index[None, :] < extents[:, 1:2])
    inside_y = (y_index[None, :] >= extents[:, 2:3]) & (y_index[None, :] < extents[:, 3:4])
    return (inside_z[:, :, None] & inside_y[:, None, :]).astype(jnp.float32)


def subject_force(image_pad, templ_pad, region_mask, in_grid, slab_depth, slab_rows):
    templ_mean, templ_var = template_stats(templ_pad, slab_depth, slab_rows)
    mean_i = box_local(image_pad, slab_depth, slab_rows) / 729.0
    square_mean = box_local(image_pad * image_pad, slab_depth, slab_rows) / 729.0
    cross_mean = box_local(image_pad * templ_pad, slab_depth, slab_rows) / 729.0
    var_i = square_mean - mean_i * mean_i + BOX_EPS
    covariance = cross_mean - mean_i * templ_mean
    image_mid = image_pad[4 : 4 + slab_depth, 4 : 4 + slab_rows, :]
    templ_mid = templ_pad[4 : 4 + slab_depth, 4 : 4 + slab_rows, :]
    centred_i = image_mid - mean_i
    centred_t = templ_mid - templ_mean
    factor = (
        region_mask
        * (2.0 * covariance / (var_i * templ_var))
        * (centred_t - covariance / var_i * centred_i)
    )
    grad_z = 0.5 * (
        image_pad[5 : 5 + slab_depth, 4 : 4 + slab_rows, :]
        - image_pad[3 : 3 + slab_depth, 4 : 4 + slab_rows, :]
    )
    grad_y = 0.5 * (
        image_pad[4 : 4 + slab_depth, 5 : 5 + slab_rows, :]
        - image_pad[4 : 4 + slab_depth, 3 : 3 + slab_rows, :]
    )
    side_pad = jnp.pad(image_mid, ((0, 0), (0, 0), (1, 1)))
    grad_x = 0.5 * (side_pad[:, :, 2:] - side_pad[:, :, :-2])
    force = jnp.stack([factor * grad_z, factor * grad_y, factor * grad_x])
    return jnp.where(in_grid[None], force, 0.0)


def local(subjects, templates, group_of, extents):
    local_subjects, slab_depth, slab_rows, cell_count = subjects.shape
    groups = templates.shape[0]
    peers = lax.axis_size("subj")
    cells = slab_depth * slab_rows * cell_count
    chunk = cells // peers
    depth_out, rows_out = (slab_depth + 2 * SPILL, slab_rows + 2 * SPILL)
    total_z, total_y = (slab_depth * lax.axis_size("gz"), slab_rows * lax.axis_size("gy"))
    first_subject = lax.axis_index("subj") * local_subjects
    subject_ids = jnp.arange(group_of.shape[0], dtype=jnp.int32)
    own_ids = first_subject + jnp.arange(local_subjects, dtype=jnp.int32)
    picks = subject_ids[None, :] == own_ids[:, None]
    own_groups = jnp.sum(jnp.where(picks, group_of[None, :], 0), axis=1)
    own_templates = jnp.broadcast_to(templates[0], subjects.shape)
    for g in range(1, groups):
        own_templates = jnp.where(
            (own_groups == g)[:, None, None, None], templates[g][None], own_templates
        )
    z_start = lax.axis_index("gz") * slab_depth
    y_start = lax.axis_index("gy") * slab_rows
    z_index = z_start + jnp.arange(slab_depth, dtype=jnp.int32)
    y_index = y_start + jnp.arange(slab_rows, dtype=jnp.int32)
    all_masks = region_masks(extents, z_index, y_index)
    own_masks = lax.dynamic_slice_in_dim(all_masks, first_subject, local_subjects)
    onehot = (group_of[:, None] == jnp.arange(groups, dtype=jnp.int32)[None, :]).astype(jnp.float32)
    counts = jnp.sum(onehot[:, :, None, None] * all_masks[:, None], axis=0)
    denominator = jnp.maximum(counts, 1.0)[..., None]

    z_wide = z_start - SPILL + jnp.arange(depth_out, dtype=jnp.int32)
    y_wide = y_start - SPILL + jnp.arange(rows_out, dtype=jnp.int32)
    wide_masks = lax.dynamic_slice_in_dim(
        region_masks(extents, z_wide, y_wide), first_subject, local_subjects
    )
    in_grid = (
        ((z_wide >= 0) & (z_wide < total_z))[:, None, None]
        & ((y_wide >= 0) & (y_wide < total_y))[None, :, None]
    )

    volumes = jnp.concatenate([own_templates, subjects], axis=0)
    padded = halo_exchange(volumes, REACH + SPILL)
    templ_all = padded[:local_subjects]
    image_all = padded[local_subjects:]
    forces = jax.vmap(
        partial(subject_force, in_grid=in_grid, slab_depth=depth_out, slab_rows=rows_out)
    )(image_all, templ_all, wide_masks[..., None])
    force_sum = jnp.sum(forces, axis=0)
    smoother = jax.vmap(partial(smooth_local, slab_depth=slab_depth, slab_rows=slab_rows))
    velocity_part = smoother(force_sum)

    masked = own_masks[..., None] * subjects
    outgoing = jnp.concatenate(
        [masked.reshape(local_subjects, peers, chunk), velocity_part.reshape(3, peers, chunk)]
    ).transpose(1, 0, 2)
    arrived = lax.all_to_all(outgoing, "subj", 0, 0, tiled=True)
    images = arrived[:, :local_subjects].reshape(peers * local_subjects, chunk)
    group_parts = [
        jnp.sum(jnp.where((group_of == g)[:, None], images, 0.0), axis=0) for g in range(groups)
    ]
    velocity_chunk = jnp.sum(arrived[:, local_subjects:], axis=0)
    own_chunk = lax.axis_index("subj") * chunk
    spread = jnp.broadcast_to(denominator, templates.shape).reshape(groups, cells)
    chunk_denominator = lax.dynamic_slice_in_dim(spread, own_chunk, chunk, axis=1)
    reduced = jnp.concatenate([jnp.stack(group_parts) / chunk_denominator, velocity_chunk])
    lanes = 128 if reduced.size % 128 == 0 else reduced.shape[-1]
    flat = reduced.reshape(-1, lanes)
    copies = jnp.broadcast_to(flat[None], (peers,) + flat.shape)
    gathered = lax.all_to_all(copies, "subj", 0, 0, tiled=True)
    gathered = gathered.reshape((peers,) + reduced.shape).transpose(1, 0, 2)
    template_sum = gathered[:groups].reshape(templates.shape)
    new_templates = template_sum
    velocity = gathered[groups:].reshape(3, slab_depth, slab_rows, cell_count)
    return (new_templates, velocity)


def solution(mesh):
    in_specs = (P("subj", "gz", "gy", None), P(None, "gz", "gy", None), P(), P())
    out_specs = (P(None, "gz", "gy", None), P(None, "gz", "gy", None))
    return jax.shard_map(local, mesh=mesh, in_specs=in_specs, out_specs=out_specs, check_vma=False)
```

```python
from functools import partial
from functools import reduce

import jax
import jax.numpy as jnp
from jax import lax
from jax.sharding import PartitionSpec as P

BOX_EPS = 1e-05
SPREAD = (0.0625, 0.25, 0.375, 0.25, 0.0625)
REACH = 4
SPILL = 2


def rim(x, side, dim, width):
    length = x.shape[dim]
    if side < 0:
        return lax.slice_in_dim(x, length - width, length, axis=dim)
    if side > 0:
        return lax.slice_in_dim(x, 0, width, axis=dim)
    return x


def shift(piece, axis, upward):
    peers = lax.axis_size(axis)
    pairs = [(i, i + 1) for i in range(peers - 1)]
    if not upward:
        pairs = [(j, i) for i, j in pairs]
    return lax.ppermute(piece, axis, pairs)


def halo_exchange(x, width):
    top = shift(rim(x, -1, 1, width), "gz", True)
    bottom = shift(rim(x, 1, 1, width), "gz", False)
    left = shift(rim(x, -1, 2, width), "gy", True)
    right = shift(rim(x, 1, 2, width), "gy", False)
    rows = jnp.stack([top, bottom])
    corner_left = shift(rim(rows, -1, 3, width), "gy", True)
    corner_right = shift(rim(rows, 1, 3, width), "gy", False)
    bands = [
        jnp.concatenate([corner_left[0], top, corner_right[0]], axis=2),
        jnp.concatenate([left, x, right], axis=2),
        jnp.concatenate([corner_left[1], bottom, corner_right[1]], axis=2),
    ]
    return jnp.concatenate(bands, axis=1)


def add_pair(former, latter):
    return former + latter


def window_sum(volume, along_axis, length, extent):
    inner = volume.shape[along_axis] - 2
    triple = reduce(
        add_pair,
        [lax.slice_in_dim(volume, offset, offset + inner, axis=along_axis) for offset in range(3)],
    )
    pieces = [
        lax.slice_in_dim(triple, offset, offset + length, axis=along_axis)
        for offset in range(0, extent, 3)
    ]
    return reduce(add_pair, pieces)


def weighted(volume, along_axis, length):
    pieces = [
        SPREAD[offset] * lax.slice_in_dim(volume, offset, offset + length, axis=along_axis)
        for offset in range(5)
    ]
    return reduce(add_pair, pieces)


def box_local(padded, slab_depth, slab_rows):
    along_z = window_sum(padded, 0, slab_depth, 9)
    along_y = window_sum(along_z, 1, slab_rows, 9)
    widened = jnp.pad(along_y, ((0, 0), (0, 0), (4, 4)))
    return window_sum(widened, 2, padded.shape[2], 9)


def smooth_local(padded, slab_depth, slab_rows):
    along_z = weighted(padded, 0, slab_depth)
    along_y = weighted(along_z, 1, slab_rows)
    widened = jnp.pad(along_y, ((0, 0), (0, 0), (2, 2)))
    return weighted(widened, 2, padded.shape[2])


def template_stats(templ_pad, slab_depth, slab_rows):
    templ_mean = box_local(templ_pad, slab_depth, slab_rows) / 729.0
    templ_var = (
        box_local(templ_pad * templ_pad, slab_depth, slab_rows) / 729.0
        - templ_mean * templ_mean
        + BOX_EPS
    )
    return (templ_mean, templ_var)


def region_masks(extents, z_index, y_index):
    inside_z = (z_index[None, :] >= extents[:, 0:1]) & (z_index[None, :] < extents[:, 1:2])
    inside_y = (y_index[None, :] >= extents[:, 2:3]) & (y_index[None, :] < extents[:, 3:4])
    return (inside_z[:, :, None] & inside_y[:, None, :]).astype(jnp.float32)


def subject_force(image_pad, templ_pad, region_mask, in_grid, slab_depth, slab_rows):
    templ_mean, templ_var = template_stats(templ_pad, slab_depth, slab_rows)
    mean_i = box_local(image_pad, slab_depth, slab_rows) / 729.0
    square_mean = box_local(image_pad * image_pad, slab_depth, slab_rows) / 729.0
    cross_mean = box_local(image_pad * templ_pad, slab_depth, slab_rows) / 729.0
    var_i = square_mean - mean_i * mean_i + BOX_EPS
    covariance = cross_mean - mean_i * templ_mean
    image_mid = image_pad[4 : 4 + slab_depth, 4 : 4 + slab_rows, :]
    templ_mid = templ_pad[4 : 4 + slab_depth, 4 : 4 + slab_rows, :]
    centred_i = image_mid - mean_i
    centred_t = templ_mid - templ_mean
    factor = (
        region_mask
        * (2.0 * covariance / (var_i * templ_var))
        * (centred_t - covariance / var_i * centred_i)
    )
    grad_z = 0.5 * (
        image_pad[5 : 5 + slab_depth, 4 : 4 + slab_rows, :]
        - image_pad[3 : 3 + slab_depth, 4 : 4 + slab_rows, :]
    )
    grad_y = 0.5 * (
        image_pad[4 : 4 + slab_depth, 5 : 5 + slab_rows, :]
        - image_pad[4 : 4 + slab_depth, 3 : 3 + slab_rows, :]
    )
    side_pad = jnp.pad(image_mid, ((0, 0), (0, 0), (1, 1)))
    grad_x = 0.5 * (side_pad[:, :, 2:] - side_pad[:, :, :-2])
    force = jnp.stack([factor * grad_z, factor * grad_y, factor * grad_x])
    return jnp.where(in_grid[None], force, 0.0)


def local(subjects, templates, group_of, extents):
    local_subjects, slab_depth, slab_rows, cell_count = subjects.shape
    groups = templates.shape[0]
    peers = lax.axis_size("subj")
    cells = slab_depth * slab_rows * cell_count
    chunk = cells // peers
    depth_out, rows_out = (slab_depth + 2 * SPILL, slab_rows + 2 * SPILL)
    total_z, total_y = (slab_depth * lax.axis_size("gz"), slab_rows * lax.axis_size("gy"))
    first_subject = lax.axis_index("subj") * local_subjects
    subject_ids = jnp.arange(group_of.shape[0], dtype=jnp.int32)
    own_ids = first_subject + jnp.arange(local_subjects, dtype=jnp.int32)
    picks = subject_ids[None, :] == own_ids[:, None]
    own_groups = jnp.sum(jnp.where(picks, group_of[None, :], 0), axis=1)
    own_templates = jnp.broadcast_to(templates[0], subjects.shape)
    for g in range(1, groups):
        own_templates = jnp.where(
            (own_groups == g)[:, None, None, None], templates[g][None], own_templates
        )
    z_start = lax.axis_index("gz") * slab_depth
    y_start = lax.axis_index("gy") * slab_rows
    z_index = z_start + jnp.arange(slab_depth, dtype=jnp.int32)
    y_index = y_start + jnp.arange(slab_rows, dtype=jnp.int32)
    all_masks = region_masks(extents, z_index, y_index)
    own_masks = lax.dynamic_slice_in_dim(all_masks, first_subject, local_subjects)
    onehot = (group_of[:, None] == jnp.arange(groups, dtype=jnp.int32)[None, :]).astype(jnp.float32)
    counts = jnp.sum(onehot[:, :, None, None] * all_masks[:, None], axis=0)
    denominator = jnp.maximum(counts, 1.0)[..., None]

    z_wide = z_start - SPILL + jnp.arange(depth_out, dtype=jnp.int32)
    y_wide = y_start - SPILL + jnp.arange(rows_out, dtype=jnp.int32)
    wide_masks = lax.dynamic_slice_in_dim(
        region_masks(extents, z_wide, y_wide), first_subject, local_subjects
    )
    in_grid = (
        ((z_wide >= 0) & (z_wide < total_z))[:, None, None]
        & ((y_wide >= 0) & (y_wide < total_y))[None, :, None]
    )

    volumes = jnp.concatenate([own_templates, subjects], axis=0)
    padded = halo_exchange(volumes, REACH + SPILL)
    templ_all = padded[:local_subjects]
    image_all = padded[local_subjects:]
    forces = jax.vmap(
        partial(subject_force, in_grid=in_grid, slab_depth=depth_out, slab_rows=rows_out)
    )(image_all, templ_all, wide_masks[..., None])
    force_sum = jnp.sum(forces, axis=0)
    smoother = jax.vmap(partial(smooth_local, slab_depth=slab_depth, slab_rows=slab_rows))
    velocity_part = smoother(force_sum)

    masked = own_masks[..., None] * subjects
    outgoing = jnp.concatenate(
        [masked.reshape(local_subjects, peers, chunk), velocity_part.reshape(3, peers, chunk)]
    ).transpose(1, 0, 2)
    arrived = lax.all_to_all(outgoing, "subj", 0, 0, tiled=True)
    images = arrived[:, :local_subjects].reshape(peers * local_subjects, chunk)
    group_parts = [
        jnp.sum(jnp.where((group_of == g)[:, None], images, 0.0), axis=0) for g in range(groups)
    ]
    velocity_chunk = jnp.sum(arrived[:, local_subjects:], axis=0)
    own_chunk = lax.axis_index("subj") * chunk
    spread = jnp.broadcast_to(denominator, templates.shape).reshape(groups, cells)
    chunk_denominator = lax.dynamic_slice_in_dim(spread, own_chunk, chunk, axis=1)
    reduced = jnp.concatenate([jnp.stack(group_parts) / chunk_denominator, velocity_chunk])
    lanes = 128 if reduced.size % 128 == 0 else reduced.shape[-1]
    flat = reduced.reshape(-1, lanes)
    copies = jnp.broadcast_to(flat[None], (peers,) + flat.shape)
    gathered = lax.all_to_all(copies, "subj", 0, 0, tiled=True)
    gathered = gathered.reshape((peers,) + reduced.shape).transpose(1, 0, 2)
    template_sum = gathered[:groups].reshape(templates.shape)
    new_templates = template_sum
    velocity = gathered[groups:].reshape(3, slab_depth, slab_rows, cell_count)
    return (new_templates, velocity)


def solution(mesh):
    in_specs = (P("subj", "gz", "gy", None), P(None, "gz", "gy", None), P(), P())
    out_specs = (P(None, "gz", "gy", None), P(None, "gz", "gy", None))
    return jax.shard_map(local, mesh=mesh, in_specs=in_specs, out_specs=out_specs, check_vma=False)
```

```python
from functools import partial
from functools import reduce

import jax
import jax.numpy as jnp
from jax import lax
from jax.sharding import PartitionSpec as P

BOX_EPS = 1e-05
SPREAD = (0.0625, 0.25, 0.375, 0.25, 0.0625)
REACH = 4
SPILL = 2


def rim(x, side, dim, width):
    length = x.shape[dim]
    if side < 0:
        return lax.slice_in_dim(x, length - width, length, axis=dim)
    if side > 0:
        return lax.slice_in_dim(x, 0, width, axis=dim)
    return x


def shift(piece, axis, upward):
    peers = lax.axis_size(axis)
    pairs = [(i, i + 1) for i in range(peers - 1)]
    if not upward:
        pairs = [(j, i) for i, j in pairs]
    return lax.ppermute(piece, axis, pairs)


def halo_exchange(x, width, edge):
    top = shift(edge(-1, 1), "gz", True)
    bottom = shift(edge(1, 1), "gz", False)
    left = shift(edge(-1, 2), "gy", True)
    right = shift(edge(1, 2), "gy", False)
    rows = jnp.stack([top, bottom])
    corner_left = shift(rim(rows, -1, 3, width), "gy", True)
    corner_right = shift(rim(rows, 1, 3, width), "gy", False)
    bands = [
        jnp.concatenate([corner_left[0], top, corner_right[0]], axis=2),
        jnp.concatenate([left, x, right], axis=2),
        jnp.concatenate([corner_left[1], bottom, corner_right[1]], axis=2),
    ]
    return jnp.concatenate(bands, axis=1)


def add_pair(former, latter):
    return former + latter


def window_sum(volume, along_axis, length, extent):
    inner = volume.shape[along_axis] - 2
    triple = reduce(
        add_pair,
        [lax.slice_in_dim(volume, offset, offset + inner, axis=along_axis) for offset in range(3)],
    )
    pieces = [
        lax.slice_in_dim(triple, offset, offset + length, axis=along_axis)
        for offset in range(0, extent, 3)
    ]
    return reduce(add_pair, pieces)


def weighted(volume, along_axis, length):
    pieces = [
        SPREAD[offset] * lax.slice_in_dim(volume, offset, offset + length, axis=along_axis)
        for offset in range(5)
    ]
    return reduce(add_pair, pieces)


def box_local(padded, slab_depth, slab_rows):
    along_z = window_sum(padded, 0, slab_depth, 9)
    along_y = window_sum(along_z, 1, slab_rows, 9)
    widened = jnp.pad(along_y, ((0, 0), (0, 0), (4, 4)))
    return window_sum(widened, 2, padded.shape[2], 9)


def smooth_local(padded, slab_depth, slab_rows):
    along_z = weighted(padded, 0, slab_depth)
    along_y = weighted(along_z, 1, slab_rows)
    widened = jnp.pad(along_y, ((0, 0), (0, 0), (2, 2)))
    return weighted(widened, 2, padded.shape[2])


def template_stats(templ_pad, slab_depth, slab_rows):
    templ_mean = box_local(templ_pad, slab_depth, slab_rows) / 729.0
    templ_var = (
        box_local(templ_pad * templ_pad, slab_depth, slab_rows) / 729.0
        - templ_mean * templ_mean
        + BOX_EPS
    )
    return (templ_mean, templ_var)


def region_masks(extents, z_index, y_index):
    inside_z = (z_index[None, :] >= extents[:, 0:1]) & (z_index[None, :] < extents[:, 1:2])
    inside_y = (y_index[None, :] >= extents[:, 2:3]) & (y_index[None, :] < extents[:, 3:4])
    return (inside_z[:, :, None] & inside_y[:, None, :]).astype(jnp.float32)


def subject_force(image_pad, templ_pad, region_mask, in_grid, slab_depth, slab_rows):
    templ_mean, templ_var = template_stats(templ_pad, slab_depth, slab_rows)
    mean_i = box_local(image_pad, slab_depth, slab_rows) / 729.0
    square_mean = box_local(image_pad * image_pad, slab_depth, slab_rows) / 729.0
    cross_mean = box_local(image_pad * templ_pad, slab_depth, slab_rows) / 729.0
    var_i = square_mean - mean_i * mean_i + BOX_EPS
    covariance = cross_mean - mean_i * templ_mean
    image_mid = image_pad[4 : 4 + slab_depth, 4 : 4 + slab_rows, :]
    templ_mid = templ_pad[4 : 4 + slab_depth, 4 : 4 + slab_rows, :]
    centred_i = image_mid - mean_i
    centred_t = templ_mid - templ_mean
    factor = (
        region_mask
        * (2.0 * covariance / (var_i * templ_var))
        * (centred_t - covariance / var_i * centred_i)
    )
    grad_z = 0.5 * (
        image_pad[5 : 5 + slab_depth, 4 : 4 + slab_rows, :]
        - image_pad[3 : 3 + slab_depth, 4 : 4 + slab_rows, :]
    )
    grad_y = 0.5 * (
        image_pad[4 : 4 + slab_depth, 5 : 5 + slab_rows, :]
        - image_pad[4 : 4 + slab_depth, 3 : 3 + slab_rows, :]
    )
    side_pad = jnp.pad(image_mid, ((0, 0), (0, 0), (1, 1)))
    grad_x = 0.5 * (side_pad[:, :, 2:] - side_pad[:, :, :-2])
    force = jnp.stack([factor * grad_z, factor * grad_y, factor * grad_x])
    return jnp.where(in_grid[None], force, 0.0)


def local(subjects, templates, group_of, extents):
    local_subjects, slab_depth, slab_rows, cell_count = subjects.shape
    groups = templates.shape[0]
    peers = lax.axis_size("subj")
    cells = slab_depth * slab_rows * cell_count
    chunk = cells // peers
    depth_out, rows_out = (slab_depth + 2 * SPILL, slab_rows + 2 * SPILL)
    total_z, total_y = (slab_depth * lax.axis_size("gz"), slab_rows * lax.axis_size("gy"))
    first_subject = lax.axis_index("subj") * local_subjects
    subject_ids = jnp.arange(group_of.shape[0], dtype=jnp.int32)
    own_ids = first_subject + jnp.arange(local_subjects, dtype=jnp.int32)
    picks = subject_ids[None, :] == own_ids[:, None]
    own_groups = jnp.sum(jnp.where(picks, group_of[None, :], 0), axis=1)
    own_templates = jnp.broadcast_to(templates[0], subjects.shape)
    for g in range(1, groups):
        own_templates = jnp.where(
            (own_groups == g)[:, None, None, None], templates[g][None], own_templates
        )
    z_start = lax.axis_index("gz") * slab_depth
    y_start = lax.axis_index("gy") * slab_rows
    z_index = z_start + jnp.arange(slab_depth, dtype=jnp.int32)
    y_index = y_start + jnp.arange(slab_rows, dtype=jnp.int32)
    all_masks = region_masks(extents, z_index, y_index)
    own_masks = lax.dynamic_slice_in_dim(all_masks, first_subject, local_subjects)
    onehot = (group_of[:, None] == jnp.arange(groups, dtype=jnp.int32)[None, :]).astype(jnp.float32)
    counts = jnp.sum(onehot[:, :, None, None] * all_masks[:, None], axis=0)
    denominator = jnp.maximum(counts, 1.0)[..., None]

    z_wide = z_start - SPILL + jnp.arange(depth_out, dtype=jnp.int32)
    y_wide = y_start - SPILL + jnp.arange(rows_out, dtype=jnp.int32)
    wide_masks = lax.dynamic_slice_in_dim(
        region_masks(extents, z_wide, y_wide), first_subject, local_subjects
    )
    in_grid = (
        ((z_wide >= 0) & (z_wide < total_z))[:, None, None]
        & ((y_wide >= 0) & (y_wide < total_y))[None, :, None]
    )

    volumes = jnp.concatenate([own_templates, subjects], axis=0)

    def edge(side, dim):
        rims = rim(templates, side, dim, REACH + SPILL)
        chosen = jnp.broadcast_to(rims[0], (local_subjects,) + rims.shape[1:])
        for g in range(1, groups):
            chosen = jnp.where((own_groups == g)[:, None, None, None], rims[g][None], chosen)
        return jnp.concatenate([chosen, rim(subjects, side, dim, REACH + SPILL)], axis=0)

    padded = halo_exchange(volumes, REACH + SPILL, edge)
    templ_all = padded[:local_subjects]
    image_all = padded[local_subjects:]
    forces = jax.vmap(
        partial(subject_force, in_grid=in_grid, slab_depth=depth_out, slab_rows=rows_out)
    )(image_all, templ_all, wide_masks[..., None])
    force_sum = jnp.sum(forces, axis=0)
    smoother = jax.vmap(partial(smooth_local, slab_depth=slab_depth, slab_rows=slab_rows))
    velocity_part = smoother(force_sum)

    masked = own_masks[..., None] * subjects
    outgoing = jnp.concatenate(
        [masked.reshape(local_subjects, peers, chunk), velocity_part.reshape(3, peers, chunk)]
    ).transpose(1, 0, 2)
    arrived = lax.all_to_all(outgoing, "subj", 0, 0, tiled=True)
    images = arrived[:, :local_subjects].reshape(peers * local_subjects, chunk)
    group_parts = [
        jnp.sum(jnp.where((group_of == g)[:, None], images, 0.0), axis=0) for g in range(groups)
    ]
    velocity_chunk = jnp.sum(arrived[:, local_subjects:], axis=0)
    own_chunk = lax.axis_index("subj") * chunk
    spread = jnp.broadcast_to(denominator, templates.shape).reshape(groups, cells)
    chunk_denominator = lax.dynamic_slice_in_dim(spread, own_chunk, chunk, axis=1)
    reduced = jnp.concatenate([jnp.stack(group_parts) / chunk_denominator, velocity_chunk])
    lanes = 128 if reduced.size % 128 == 0 else reduced.shape[-1]
    flat = reduced.reshape(-1, lanes)
    copies = jnp.broadcast_to(flat[None], (peers,) + flat.shape)
    gathered = lax.all_to_all(copies, "subj", 0, 0, tiled=True)
    gathered = gathered.reshape((peers,) + reduced.shape).transpose(1, 0, 2)
    template_sum = gathered[:groups].reshape(templates.shape)
    new_templates = template_sum
    velocity = gathered[groups:].reshape(3, slab_depth, slab_rows, cell_count)
    return (new_templates, velocity)


def solution(mesh):
    in_specs = (P("subj", "gz", "gy", None), P(None, "gz", "gy", None), P(), P())
    out_specs = (P(None, "gz", "gy", None), P(None, "gz", "gy", None))
    return jax.shard_map(local, mesh=mesh, in_specs=in_specs, out_specs=out_specs, check_vma=False)
```

```python
from functools import partial
from functools import reduce

import jax
import jax.numpy as jnp
from jax import lax
from jax.sharding import PartitionSpec as P

BOX_EPS = 1e-05
SPREAD = (0.0625, 0.25, 0.375, 0.25, 0.0625)
REACH = 4
SPILL = 2


def rim(x, side, dim, width):
    length = x.shape[dim]
    if side < 0:
        return lax.slice_in_dim(x, length - width, length, axis=dim)
    if side > 0:
        return lax.slice_in_dim(x, 0, width, axis=dim)
    return x


def shift(piece, axis, upward):
    peers = lax.axis_size(axis)
    pairs = [(i, i + 1) for i in range(peers - 1)]
    if not upward:
        pairs = [(j, i) for i, j in pairs]
    return lax.ppermute(piece, axis, pairs)


def halo_exchange(x, width, edge):
    top = shift(edge(-1, 1), "gz", True)
    bottom = shift(edge(1, 1), "gz", False)
    left = shift(edge(-1, 2), "gy", True)
    right = shift(edge(1, 2), "gy", False)
    rows = jnp.stack([top, bottom])
    corner_left = shift(rim(rows, -1, 3, width), "gy", True)
    corner_right = shift(rim(rows, 1, 3, width), "gy", False)
    bands = [
        jnp.concatenate([corner_left[0], top, corner_right[0]], axis=2),
        jnp.concatenate([left, x, right], axis=2),
        jnp.concatenate([corner_left[1], bottom, corner_right[1]], axis=2),
    ]
    return jnp.concatenate(bands, axis=1)


def add_pair(former, latter):
    return former + latter


def window_sum(volume, along_axis, length, extent):
    inner = volume.shape[along_axis] - 2
    triple = reduce(
        add_pair,
        [lax.slice_in_dim(volume, offset, offset + inner, axis=along_axis) for offset in range(3)],
    )
    pieces = [
        lax.slice_in_dim(triple, offset, offset + length, axis=along_axis)
        for offset in range(0, extent, 3)
    ]
    return reduce(add_pair, pieces)


def weighted(volume, along_axis, length):
    pieces = [
        SPREAD[offset] * lax.slice_in_dim(volume, offset, offset + length, axis=along_axis)
        for offset in range(5)
    ]
    return reduce(add_pair, pieces)


def box_local(padded, slab_depth, slab_rows):
    along_z = window_sum(padded, 0, slab_depth, 9)
    along_y = window_sum(along_z, 1, slab_rows, 9)
    widened = jnp.pad(along_y, ((0, 0), (0, 0), (4, 4)))
    return window_sum(widened, 2, padded.shape[2], 9)


def smooth_local(padded, slab_depth, slab_rows):
    along_z = weighted(padded, 0, slab_depth)
    along_y = weighted(along_z, 1, slab_rows)
    widened = jnp.pad(along_y, ((0, 0), (0, 0), (2, 2)))
    return weighted(widened, 2, padded.shape[2])


def template_stats(templ_pad, slab_depth, slab_rows):
    templ_mean = box_local(templ_pad, slab_depth, slab_rows) / 729.0
    templ_var = (
        box_local(templ_pad * templ_pad, slab_depth, slab_rows) / 729.0
        - templ_mean * templ_mean
        + BOX_EPS
    )
    return (templ_mean, templ_var)


def region_masks(extents, z_index, y_index):
    inside_z = (z_index[None, :] >= extents[:, 0:1]) & (z_index[None, :] < extents[:, 1:2])
    inside_y = (y_index[None, :] >= extents[:, 2:3]) & (y_index[None, :] < extents[:, 3:4])
    return (inside_z[:, :, None] & inside_y[:, None, :]).astype(jnp.float32)


def subject_force(image_pad, templ_pad, region_mask, in_grid, slab_depth, slab_rows):
    templ_mean, templ_var = template_stats(templ_pad, slab_depth, slab_rows)
    mean_i = box_local(image_pad, slab_depth, slab_rows) / 729.0
    square_mean = box_local(image_pad * image_pad, slab_depth, slab_rows) / 729.0
    cross_mean = box_local(image_pad * templ_pad, slab_depth, slab_rows) / 729.0
    var_i = square_mean - mean_i * mean_i + BOX_EPS
    covariance = cross_mean - mean_i * templ_mean
    image_mid = image_pad[4 : 4 + slab_depth, 4 : 4 + slab_rows, :]
    templ_mid = templ_pad[4 : 4 + slab_depth, 4 : 4 + slab_rows, :]
    centred_i = image_mid - mean_i
    centred_t = templ_mid - templ_mean
    factor = (
        region_mask
        * (2.0 * covariance / (var_i * templ_var))
        * (centred_t - covariance / var_i * centred_i)
    )
    grad_z = 0.5 * (
        image_pad[5 : 5 + slab_depth, 4 : 4 + slab_rows, :]
        - image_pad[3 : 3 + slab_depth, 4 : 4 + slab_rows, :]
    )
    grad_y = 0.5 * (
        image_pad[4 : 4 + slab_depth, 5 : 5 + slab_rows, :]
        - image_pad[4 : 4 + slab_depth, 3 : 3 + slab_rows, :]
    )
    side_pad = jnp.pad(image_mid, ((0, 0), (0, 0), (1, 1)))
    grad_x = 0.5 * (side_pad[:, :, 2:] - side_pad[:, :, :-2])
    force = jnp.stack([factor * grad_z, factor * grad_y, factor * grad_x])
    return jnp.where(in_grid[None], force, 0.0)


def local(subjects, templates, group_of, extents):
    local_subjects, slab_depth, slab_rows, cell_count = subjects.shape
    groups = templates.shape[0]
    peers = lax.axis_size("subj")
    cells = slab_depth * slab_rows * cell_count
    chunk = cells // peers
    depth_out, rows_out = (slab_depth + 2 * SPILL, slab_rows + 2 * SPILL)
    total_z, total_y = (slab_depth * lax.axis_size("gz"), slab_rows * lax.axis_size("gy"))
    first_subject = lax.axis_index("subj") * local_subjects
    subject_ids = jnp.arange(group_of.shape[0], dtype=jnp.int32)
    own_ids = first_subject + jnp.arange(local_subjects, dtype=jnp.int32)
    picks = subject_ids[None, :] == own_ids[:, None]
    own_groups = jnp.sum(jnp.where(picks, group_of[None, :], 0), axis=1)
    own_templates = jnp.broadcast_to(templates[0], subjects.shape)
    for g in range(1, groups):
        own_templates = jnp.where(
            (own_groups == g)[:, None, None, None], templates[g][None], own_templates
        )
    z_start = lax.axis_index("gz") * slab_depth
    y_start = lax.axis_index("gy") * slab_rows
    z_index = z_start + jnp.arange(slab_depth, dtype=jnp.int32)
    y_index = y_start + jnp.arange(slab_rows, dtype=jnp.int32)
    all_masks = region_masks(extents, z_index, y_index)
    own_masks = lax.dynamic_slice_in_dim(all_masks, first_subject, local_subjects)
    onehot = (group_of[:, None] == jnp.arange(groups, dtype=jnp.int32)[None, :]).astype(jnp.float32)
    counts = jnp.sum(onehot[:, :, None, None] * all_masks[:, None], axis=0)
    denominator = jnp.maximum(counts, 1.0)[..., None]

    z_wide = z_start - SPILL + jnp.arange(depth_out, dtype=jnp.int32)
    y_wide = y_start - SPILL + jnp.arange(rows_out, dtype=jnp.int32)
    wide_masks = lax.dynamic_slice_in_dim(
        region_masks(extents, z_wide, y_wide), first_subject, local_subjects
    )
    in_grid = (
        ((z_wide >= 0) & (z_wide < total_z))[:, None, None]
        & ((y_wide >= 0) & (y_wide < total_y))[None, :, None]
    )

    volumes = jnp.concatenate([own_templates, subjects], axis=0)

    def edge(side, dim):
        rims = rim(templates, side, dim, REACH + SPILL)
        chosen = jnp.broadcast_to(rims[0], (local_subjects,) + rims.shape[1:])
        for g in range(1, groups):
            chosen = jnp.where((own_groups == g)[:, None, None, None], rims[g][None], chosen)
        return jnp.concatenate([chosen, rim(subjects, side, dim, REACH + SPILL)], axis=0)

    padded = halo_exchange(volumes, REACH + SPILL, edge)
    templ_all = padded[:local_subjects]
    image_all = padded[local_subjects:]
    forces = jax.vmap(
        partial(subject_force, in_grid=in_grid, slab_depth=depth_out, slab_rows=rows_out)
    )(image_all, templ_all, wide_masks[..., None])
    force_sum = jnp.sum(forces, axis=0)
    smoother = jax.vmap(partial(smooth_local, slab_depth=slab_depth, slab_rows=slab_rows))
    velocity_part = smoother(force_sum)

    masked = own_masks[..., None] * subjects
    outgoing = jnp.stack(
        [masked[l].reshape(peers, chunk) for l in range(local_subjects)]
        + [velocity_part[c].reshape(peers, chunk) for c in range(3)],
        axis=1,
    )
    arrived = lax.all_to_all(outgoing, "subj", 0, 0, tiled=True)
    images = arrived[:, :local_subjects].reshape(peers * local_subjects, chunk)
    group_parts = [
        jnp.sum(jnp.where((group_of == g)[:, None], images, 0.0), axis=0) for g in range(groups)
    ]
    velocity_chunk = jnp.sum(arrived[:, local_subjects:], axis=0)
    own_chunk = lax.axis_index("subj") * chunk
    spread = jnp.broadcast_to(denominator, templates.shape).reshape(groups, cells)
    chunk_denominator = lax.dynamic_slice_in_dim(spread, own_chunk, chunk, axis=1)
    reduced = jnp.concatenate([jnp.stack(group_parts) / chunk_denominator, velocity_chunk])
    lanes = 128 if reduced.size % 128 == 0 else reduced.shape[-1]
    flat = reduced.reshape(-1, lanes)
    copies = jnp.broadcast_to(flat[None], (peers,) + flat.shape)
    gathered = lax.all_to_all(copies, "subj", 0, 0, tiled=True)
    gathered = gathered.reshape((peers,) + reduced.shape).transpose(1, 0, 2)
    template_sum = gathered[:groups].reshape(templates.shape)
    new_templates = template_sum
    velocity = gathered[groups:].reshape(3, slab_depth, slab_rows, cell_count)
    return (new_templates, velocity)


def solution(mesh):
    in_specs = (P("subj", "gz", "gy", None), P(None, "gz", "gy", None), P(), P())
    out_specs = (P(None, "gz", "gy", None), P(None, "gz", "gy", None))
    return jax.shard_map(local, mesh=mesh, in_specs=in_specs, out_specs=out_specs, check_vma=False)
```

```python
from functools import partial
from functools import reduce

import jax
import jax.numpy as jnp
from jax import lax
from jax.sharding import PartitionSpec as P

BOX_EPS = 1e-05
SPREAD = (0.0625, 0.25, 0.375, 0.25, 0.0625)
REACH = 4
SPILL = 2


def rim(x, side, dim, width):
    length = x.shape[dim]
    if side < 0:
        return lax.slice_in_dim(x, length - width, length, axis=dim)
    if side > 0:
        return lax.slice_in_dim(x, 0, width, axis=dim)
    return x


def shift(piece, axis, upward):
    peers = lax.axis_size(axis)
    pairs = [(i, i + 1) for i in range(peers - 1)]
    if not upward:
        pairs = [(j, i) for i, j in pairs]
    return lax.ppermute(piece, axis, pairs)


def halo_exchange(x, width, edge):
    top = shift(edge(-1, 1), "gz", True)
    bottom = shift(edge(1, 1), "gz", False)
    left = shift(edge(-1, 2), "gy", True)
    right = shift(edge(1, 2), "gy", False)
    rows = jnp.stack([top, bottom])
    corner_left = shift(rim(rows, -1, 3, width), "gy", True)
    corner_right = shift(rim(rows, 1, 3, width), "gy", False)
    bands = [
        jnp.concatenate([corner_left[0], top, corner_right[0]], axis=2),
        jnp.concatenate([left, x, right], axis=2),
        jnp.concatenate([corner_left[1], bottom, corner_right[1]], axis=2),
    ]
    return jnp.concatenate(bands, axis=1)


def add_pair(former, latter):
    return former + latter


def window_sum(volume, along_axis, length, extent):
    inner = volume.shape[along_axis] - 2
    triple = reduce(
        add_pair,
        [lax.slice_in_dim(volume, offset, offset + inner, axis=along_axis) for offset in range(3)],
    )
    pieces = [
        lax.slice_in_dim(triple, offset, offset + length, axis=along_axis)
        for offset in range(0, extent, 3)
    ]
    return reduce(add_pair, pieces)


def weighted(volume, along_axis, length):
    pieces = [
        SPREAD[offset] * lax.slice_in_dim(volume, offset, offset + length, axis=along_axis)
        for offset in range(5)
    ]
    return reduce(add_pair, pieces)


def box_local(padded, slab_depth, slab_rows):
    along_z = window_sum(padded, 0, slab_depth, 9)
    along_y = window_sum(along_z, 1, slab_rows, 9)
    return lax.reduce_window(
        along_y, 0.0, lax.add, (1, 1, 9), (1, 1, 1), ((0, 0), (0, 0), (4, 4))
    )


def smooth_local(padded, slab_depth, slab_rows):
    along_z = weighted(padded, 0, slab_depth)
    along_y = weighted(along_z, 1, slab_rows)
    widened = jnp.pad(along_y, ((0, 0), (0, 0), (2, 2)))
    return weighted(widened, 2, padded.shape[2])


def template_stats(templ_pad, slab_depth, slab_rows):
    templ_mean = box_local(templ_pad, slab_depth, slab_rows) / 729.0
    templ_var = (
        box_local(templ_pad * templ_pad, slab_depth, slab_rows) / 729.0
        - templ_mean * templ_mean
        + BOX_EPS
    )
    return (templ_mean, templ_var)


def region_masks(extents, z_index, y_index):
    inside_z = (z_index[None, :] >= extents[:, 0:1]) & (z_index[None, :] < extents[:, 1:2])
    inside_y = (y_index[None, :] >= extents[:, 2:3]) & (y_index[None, :] < extents[:, 3:4])
    return (inside_z[:, :, None] & inside_y[:, None, :]).astype(jnp.float32)


def subject_force(image_pad, templ_pad, region_mask, in_grid, slab_depth, slab_rows):
    templ_mean, templ_var = template_stats(templ_pad, slab_depth, slab_rows)
    mean_i = box_local(image_pad, slab_depth, slab_rows) / 729.0
    square_mean = box_local(image_pad * image_pad, slab_depth, slab_rows) / 729.0
    cross_mean = box_local(image_pad * templ_pad, slab_depth, slab_rows) / 729.0
    var_i = square_mean - mean_i * mean_i + BOX_EPS
    covariance = cross_mean - mean_i * templ_mean
    image_mid = image_pad[4 : 4 + slab_depth, 4 : 4 + slab_rows, :]
    templ_mid = templ_pad[4 : 4 + slab_depth, 4 : 4 + slab_rows, :]
    centred_i = image_mid - mean_i
    centred_t = templ_mid - templ_mean
    factor = (
        region_mask
        * (2.0 * covariance / (var_i * templ_var))
        * (centred_t - covariance / var_i * centred_i)
    )
    grad_z = 0.5 * (
        image_pad[5 : 5 + slab_depth, 4 : 4 + slab_rows, :]
        - image_pad[3 : 3 + slab_depth, 4 : 4 + slab_rows, :]
    )
    grad_y = 0.5 * (
        image_pad[4 : 4 + slab_depth, 5 : 5 + slab_rows, :]
        - image_pad[4 : 4 + slab_depth, 3 : 3 + slab_rows, :]
    )
    side_pad = jnp.pad(image_mid, ((0, 0), (0, 0), (1, 1)))
    grad_x = 0.5 * (side_pad[:, :, 2:] - side_pad[:, :, :-2])
    force = jnp.stack([factor * grad_z, factor * grad_y, factor * grad_x])
    return jnp.where(in_grid[None], force, 0.0)


def local(subjects, templates, group_of, extents):
    local_subjects, slab_depth, slab_rows, cell_count = subjects.shape
    groups = templates.shape[0]
    peers = lax.axis_size("subj")
    cells = slab_depth * slab_rows * cell_count
    chunk = cells // peers
    depth_out, rows_out = (slab_depth + 2 * SPILL, slab_rows + 2 * SPILL)
    total_z, total_y = (slab_depth * lax.axis_size("gz"), slab_rows * lax.axis_size("gy"))
    first_subject = lax.axis_index("subj") * local_subjects
    subject_ids = jnp.arange(group_of.shape[0], dtype=jnp.int32)
    own_ids = first_subject + jnp.arange(local_subjects, dtype=jnp.int32)
    picks = subject_ids[None, :] == own_ids[:, None]
    own_groups = jnp.sum(jnp.where(picks, group_of[None, :], 0), axis=1)
    own_templates = jnp.broadcast_to(templates[0], subjects.shape)
    for g in range(1, groups):
        own_templates = jnp.where(
            (own_groups == g)[:, None, None, None], templates[g][None], own_templates
        )
    z_start = lax.axis_index("gz") * slab_depth
    y_start = lax.axis_index("gy") * slab_rows
    z_index = z_start + jnp.arange(slab_depth, dtype=jnp.int32)
    y_index = y_start + jnp.arange(slab_rows, dtype=jnp.int32)
    all_masks = region_masks(extents, z_index, y_index)
    own_masks = lax.dynamic_slice_in_dim(all_masks, first_subject, local_subjects)
    onehot = (group_of[:, None] == jnp.arange(groups, dtype=jnp.int32)[None, :]).astype(jnp.float32)
    counts = jnp.sum(onehot[:, :, None, None] * all_masks[:, None], axis=0)
    denominator = jnp.maximum(counts, 1.0)[..., None]

    z_wide = z_start - SPILL + jnp.arange(depth_out, dtype=jnp.int32)
    y_wide = y_start - SPILL + jnp.arange(rows_out, dtype=jnp.int32)
    wide_masks = lax.dynamic_slice_in_dim(
        region_masks(extents, z_wide, y_wide), first_subject, local_subjects
    )
    in_grid = (
        ((z_wide >= 0) & (z_wide < total_z))[:, None, None]
        & ((y_wide >= 0) & (y_wide < total_y))[None, :, None]
    )

    volumes = jnp.concatenate([own_templates, subjects], axis=0)

    def edge(side, dim):
        rims = rim(templates, side, dim, REACH + SPILL)
        chosen = jnp.broadcast_to(rims[0], (local_subjects,) + rims.shape[1:])
        for g in range(1, groups):
            chosen = jnp.where((own_groups == g)[:, None, None, None], rims[g][None], chosen)
        return jnp.concatenate([chosen, rim(subjects, side, dim, REACH + SPILL)], axis=0)

    padded = halo_exchange(volumes, REACH + SPILL, edge)
    templ_all = padded[:local_subjects]
    image_all = padded[local_subjects:]
    forces = jax.vmap(
        partial(subject_force, in_grid=in_grid, slab_depth=depth_out, slab_rows=rows_out)
    )(image_all, templ_all, wide_masks[..., None])
    force_sum = jnp.sum(forces, axis=0)
    smoother = jax.vmap(partial(smooth_local, slab_depth=slab_depth, slab_rows=slab_rows))
    velocity_part = smoother(force_sum)

    masked = own_masks[..., None] * subjects
    outgoing = jnp.concatenate(
        [masked.reshape(local_subjects, peers, chunk), velocity_part.reshape(3, peers, chunk)]
    ).transpose(1, 0, 2)
    arrived = lax.all_to_all(outgoing, "subj", 0, 0, tiled=True)
    images = arrived[:, :local_subjects].reshape(peers * local_subjects, chunk)
    group_parts = [
        jnp.sum(jnp.where((group_of == g)[:, None], images, 0.0), axis=0) for g in range(groups)
    ]
    velocity_chunk = jnp.sum(arrived[:, local_subjects:], axis=0)
    own_chunk = lax.axis_index("subj") * chunk
    spread = jnp.broadcast_to(denominator, templates.shape).reshape(groups, cells)
    chunk_denominator = lax.dynamic_slice_in_dim(spread, own_chunk, chunk, axis=1)
    reduced = jnp.concatenate([jnp.stack(group_parts) / chunk_denominator, velocity_chunk])
    lanes = 128 if reduced.size % 128 == 0 else reduced.shape[-1]
    flat = reduced.reshape(-1, lanes)
    copies = jnp.broadcast_to(flat[None], (peers,) + flat.shape)
    gathered = lax.all_to_all(copies, "subj", 0, 0, tiled=True)
    gathered = gathered.reshape((peers,) + reduced.shape).transpose(1, 0, 2)
    template_sum = gathered[:groups].reshape(templates.shape)
    new_templates = template_sum
    velocity = gathered[groups:].reshape(3, slab_depth, slab_rows, cell_count)
    return (new_templates, velocity)


def solution(mesh):
    in_specs = (P("subj", "gz", "gy", None), P(None, "gz", "gy", None), P(), P())
    out_specs = (P(None, "gz", "gy", None), P(None, "gz", "gy", None))
    return jax.shard_map(local, mesh=mesh, in_specs=in_specs, out_specs=out_specs, check_vma=False)
```

```python
from functools import partial
from functools import reduce

import jax
import jax.numpy as jnp
from jax import lax
from jax.sharding import PartitionSpec as P

BOX_EPS = 1e-05
SPREAD = (0.0625, 0.25, 0.375, 0.25, 0.0625)
REACH = 4
SPILL = 2


def rim(x, side, dim, width):
    length = x.shape[dim]
    if side < 0:
        return lax.slice_in_dim(x, length - width, length, axis=dim)
    if side > 0:
        return lax.slice_in_dim(x, 0, width, axis=dim)
    return x


def shift(piece, axis, upward):
    peers = lax.axis_size(axis)
    pairs = [(i, i + 1) for i in range(peers - 1)]
    if not upward:
        pairs = [(j, i) for i, j in pairs]
    return lax.ppermute(piece, axis, pairs)


def halo_exchange(x, width, edge):
    top = shift(edge(-1, 1), "gz", True)
    bottom = shift(edge(1, 1), "gz", False)
    left = shift(edge(-1, 2), "gy", True)
    right = shift(edge(1, 2), "gy", False)
    rows = jnp.stack([top, bottom])
    corner_left = shift(rim(rows, -1, 3, width), "gy", True)
    corner_right = shift(rim(rows, 1, 3, width), "gy", False)
    bands = [
        jnp.concatenate([corner_left[0], top, corner_right[0]], axis=2),
        jnp.concatenate([left, x, right], axis=2),
        jnp.concatenate([corner_left[1], bottom, corner_right[1]], axis=2),
    ]
    return jnp.concatenate(bands, axis=1)


def add_pair(former, latter):
    return former + latter


def window_sum(volume, along_axis, length, extent):
    inner = volume.shape[along_axis] - 2
    triple = reduce(
        add_pair,
        [lax.slice_in_dim(volume, offset, offset + inner, axis=along_axis) for offset in range(3)],
    )
    pieces = [
        lax.slice_in_dim(triple, offset, offset + length, axis=along_axis)
        for offset in range(0, extent, 3)
    ]
    return reduce(add_pair, pieces)


def weighted(volume, along_axis, length):
    pieces = [
        SPREAD[offset] * lax.slice_in_dim(volume, offset, offset + length, axis=along_axis)
        for offset in range(5)
    ]
    return reduce(add_pair, pieces)


def box_local(padded, slab_depth, slab_rows):
    along_z = window_sum(padded, 0, slab_depth, 9)
    along_y = window_sum(along_z, 1, slab_rows, 9)
    widened = jnp.pad(along_y, ((0, 0), (0, 0), (4, 4)))
    return window_sum(widened, 2, padded.shape[2], 9)


def smooth_local(padded, slab_depth, slab_rows):
    along_z = weighted(padded, 0, slab_depth)
    along_y = weighted(along_z, 1, slab_rows)
    widened = jnp.pad(along_y, ((0, 0), (0, 0), (2, 2)))
    return weighted(widened, 2, padded.shape[2])


def template_stats(templ_pad, slab_depth, slab_rows):
    templ_mean = box_local(templ_pad, slab_depth, slab_rows) / 729.0
    templ_var = (
        box_local(templ_pad * templ_pad, slab_depth, slab_rows) / 729.0
        - templ_mean * templ_mean
        + BOX_EPS
    )
    return (templ_mean, templ_var)


def region_masks(extents, z_index, y_index):
    inside_z = (z_index[None, :] >= extents[:, 0:1]) & (z_index[None, :] < extents[:, 1:2])
    inside_y = (y_index[None, :] >= extents[:, 2:3]) & (y_index[None, :] < extents[:, 3:4])
    return (inside_z[:, :, None] & inside_y[:, None, :]).astype(jnp.float32)


def subject_force(image_pad, templ_pad, region_mask, in_grid, slab_depth, slab_rows):
    templ_mean, templ_var = template_stats(templ_pad, slab_depth, slab_rows)
    mean_i = box_local(image_pad, slab_depth, slab_rows) / 729.0
    square_mean = box_local(image_pad * image_pad, slab_depth, slab_rows) / 729.0
    cross_mean = box_local(image_pad * templ_pad, slab_depth, slab_rows) / 729.0
    var_i = square_mean - mean_i * mean_i + BOX_EPS
    covariance = cross_mean - mean_i * templ_mean
    image_mid = image_pad[4 : 4 + slab_depth, 4 : 4 + slab_rows, :]
    templ_mid = templ_pad[4 : 4 + slab_depth, 4 : 4 + slab_rows, :]
    centred_i = image_mid - mean_i
    centred_t = templ_mid - templ_mean
    factor = (
        region_mask
        * (2.0 * covariance / (var_i * templ_var))
        * (centred_t - covariance / var_i * centred_i)
    )
    grad_z = 0.5 * (
        image_pad[5 : 5 + slab_depth, 4 : 4 + slab_rows, :]
        - image_pad[3 : 3 + slab_depth, 4 : 4 + slab_rows, :]
    )
    grad_y = 0.5 * (
        image_pad[4 : 4 + slab_depth, 5 : 5 + slab_rows, :]
        - image_pad[4 : 4 + slab_depth, 3 : 3 + slab_rows, :]
    )
    side_pad = jnp.pad(image_mid, ((0, 0), (0, 0), (1, 1)))
    grad_x = 0.5 * (side_pad[:, :, 2:] - side_pad[:, :, :-2])
    force = jnp.stack([factor * grad_z, factor * grad_y, factor * grad_x])
    return jnp.where(in_grid[None], force, 0.0)


def local(subjects, templates, group_of, extents):
    local_subjects, slab_depth, slab_rows, cell_count = subjects.shape
    groups = templates.shape[0]
    peers = lax.axis_size("subj")
    cells = slab_depth * slab_rows * cell_count
    chunk = cells // peers
    depth_out, rows_out = (slab_depth + 2 * SPILL, slab_rows + 2 * SPILL)
    total_z, total_y = (slab_depth * lax.axis_size("gz"), slab_rows * lax.axis_size("gy"))
    first_subject = lax.axis_index("subj") * local_subjects
    subject_ids = jnp.arange(group_of.shape[0], dtype=jnp.int32)
    own_ids = first_subject + jnp.arange(local_subjects, dtype=jnp.int32)
    picks = subject_ids[None, :] == own_ids[:, None]
    own_groups = jnp.sum(jnp.where(picks, group_of[None, :], 0), axis=1)
    own_templates = jnp.broadcast_to(templates[0], subjects.shape)
    for g in range(1, groups):
        own_templates = jnp.where(
            (own_groups == g)[:, None, None, None], templates[g][None], own_templates
        )
    z_start = lax.axis_index("gz") * slab_depth
    y_start = lax.axis_index("gy") * slab_rows
    z_index = z_start + jnp.arange(slab_depth, dtype=jnp.int32)
    y_index = y_start + jnp.arange(slab_rows, dtype=jnp.int32)
    all_masks = region_masks(extents, z_index, y_index)
    own_masks = lax.dynamic_slice_in_dim(all_masks, first_subject, local_subjects)
    onehot = (group_of[:, None] == jnp.arange(groups, dtype=jnp.int32)[None, :]).astype(jnp.float32)
    counts = jnp.sum(onehot[:, :, None, None] * all_masks[:, None], axis=0)
    denominator = jnp.maximum(counts, 1.0)[..., None]

    z_wide = z_start - SPILL + jnp.arange(depth_out, dtype=jnp.int32)
    y_wide = y_start - SPILL + jnp.arange(rows_out, dtype=jnp.int32)
    wide_masks = lax.dynamic_slice_in_dim(
        region_masks(extents, z_wide, y_wide), first_subject, local_subjects
    )
    in_grid = (
        ((z_wide >= 0) & (z_wide < total_z))[:, None, None]
        & ((y_wide >= 0) & (y_wide < total_y))[None, :, None]
    )

    volumes = jnp.concatenate([own_templates, subjects], axis=0)

    def edge(side, dim):
        rims = rim(templates, side, dim, REACH + SPILL)
        chosen = jnp.broadcast_to(rims[0], (local_subjects,) + rims.shape[1:])
        for g in range(1, groups):
            chosen = jnp.where((own_groups == g)[:, None, None, None], rims[g][None], chosen)
        return jnp.concatenate([chosen, rim(subjects, side, dim, REACH + SPILL)], axis=0)

    padded = halo_exchange(volumes, REACH + SPILL, edge)
    templ_all = padded[:local_subjects]
    image_all = padded[local_subjects:]
    forces = jax.vmap(
        partial(subject_force, in_grid=in_grid, slab_depth=depth_out, slab_rows=rows_out)
    )(image_all, templ_all, wide_masks[..., None])
    force_sum = jnp.sum(forces, axis=0)
    smoother = jax.vmap(partial(smooth_local, slab_depth=slab_depth, slab_rows=slab_rows))
    velocity_part = smoother(force_sum)

    masked = own_masks[..., None] * subjects
    outgoing = jnp.concatenate(
        [masked.reshape(local_subjects, peers, chunk), velocity_part.reshape(3, peers, chunk)]
    ).transpose(1, 0, 2)
    arrived = lax.all_to_all(outgoing, "subj", 0, 0, tiled=True)
    images = arrived[:, :local_subjects].reshape(peers * local_subjects, chunk)
    group_parts = [
        jnp.sum(jnp.where((group_of == g)[:, None], images, 0.0), axis=0) for g in range(groups)
    ]
    velocity_chunk = jnp.sum(arrived[:, local_subjects:], axis=0)
    reduced = jnp.concatenate([jnp.stack(group_parts), velocity_chunk])
    lanes = 128 if reduced.size % 128 == 0 else reduced.shape[-1]
    flat = reduced.reshape(-1, lanes)
    copies = jnp.broadcast_to(flat[None], (peers,) + flat.shape)
    gathered = lax.all_to_all(copies, "subj", 0, 0, tiled=True)
    gathered = gathered.reshape((peers,) + reduced.shape).transpose(1, 0, 2)
    template_sum = gathered[:groups].reshape(templates.shape)
    new_templates = template_sum / denominator
    velocity = gathered[groups:].reshape(3, slab_depth, slab_rows, cell_count)
    return (new_templates, velocity)


def solution(mesh):
    in_specs = (P("subj", "gz", "gy", None), P(None, "gz", "gy", None), P(), P())
    out_specs = (P(None, "gz", "gy", None), P(None, "gz", "gy", None))
    return jax.shard_map(local, mesh=mesh, in_specs=in_specs, out_specs=out_specs, check_vma=False)
```
